512 devices in a mesh: row: 32 (over z, core), col: 16 (over x, y).
Axes of the slice: x: 4, y: 4, z: 16, core: 2. Of those that a mesh axis runs over, the one named last changes fastest.
Arguments:
- centroids: float32 [3, 16384], P(None, ('row', 'col')), may hold values from -4 to 4
- strengths: float32 [32, 16384], P(None, ('row', 'col')), may hold values from -6 to 6
- self_inv: float32 [32, 16384], P(None, ('row', 'col')), may hold values from -6 to 6
- wavenumbers: float32 [16], replicated, may hold values from 0.3 to 2
- field_pos: float32 [3, 8192], P(None, 'row'), may hold values from -4 to 4
- targets: float32 [32, 8192], P(None, 'row'), may hold values from -6 to 6
- lists: int32 [8192, 64], P('row'), may hold values from 0 to 16383
- connect: int32 [4, 16384], P(None, 'row'), may hold values from 0 to 16383, as said below
Outputs:
- adjoint: float32 [32, 16384], P(None, ('row', 'col'))
- vertex_sens: float32 [3, 16384], P(None, ('row', 'col'))
- objective: float32 [], replicated
The draws below stay inside these ranges and needn't reach their ends.
Inputs may be any that keep to these rules, and one draw needn't show every extreme that they name: `connect`: the four vertices of panel i lie in the block of 512 vertices that starts at i - i % 512; the first of them is i itself.
All inputs are finite; a program needn't handle non-finite values.
Results may differ from the reference program's by a relative error of at most 0.0003.
Values sent between devices are 32-bit elements; how exact they have to be, the bound alone decides.
No kernel may reach another device: no remote copies, remote signals or barrier semaphores. Data moves between devices by JAX's collectives and lax.ppermute only.
A program may use at most 64 MiB of HBM per device.

```python
import math
import jax
import jax.numpy as jnp
import numpy as np
from jax import lax

PAN_DEV = 32
NF = 16
LIST = 64
PANELS = 16384
VERTS = 16384
ROWBLOCK = 512
FIELD = 8192


def draw_connect(key, part):
    panel_index = jnp.arange(PANELS, dtype=jnp.int32)
    inside = panel_index % ROWBLOCK
    start = panel_index - inside
    steps = jax.random.randint(key, (4, PANELS), 0, 2 * PAN_DEV + 1, dtype=jnp.int32)
    corner_index = jnp.arange(4, dtype=jnp.int32)[:, None]
    steps = jnp.where(corner_index == 0, jnp.zeros_like(steps), steps)
    return start[None, :] + (inside[None, :] + steps) % ROWBLOCK


def plant(result, key, smallest, top_value):
    extent = result.shape
    spot = [jax.random.randint(jax.random.fold_in(key, axis), (), 0, extent[axis]) for axis in range(len(extent))]
    result = result.at[tuple(spot)].set(smallest)
    longest = extent.index(max(extent))
    spot[longest] = (spot[longest] + 1) % extent[longest]
    return result.at[tuple(spot)].set(top_value)


def levels(stream_key, shape, pieces, smallest, high):
    gain, own = 1.0, jax.random.fold_in(stream_key, 6)
    for position, blocks in pieces:
        heights = jnp.exp(jax.random.uniform(jax.random.fold_in(own, position), (blocks,), jnp.float32, smallest / len(pieces), high / len(pieces)))
        gain = gain * jnp.repeat(heights, shape[position] // blocks).reshape([-1 if axis == position else 1 for axis in range(len(shape))])
    return gain


def rank_bounds(number_of, skew):
    weights = [(1 << 20) // math.isqrt(rank ** skew) + 1 for rank in range(1, number_of + 1)]
    spread = 1 + sum(weights) // (1 << 30)
    return np.cumsum(np.array([max(1, weight // spread) for weight in weights]))


def ranked(key, extent, number_of, slope):
    table = rank_bounds(number_of, slope)
    pick = jax.random.randint(jax.random.fold_in(key, 1), extent, 0, int(table[number_of - 1]))
    grade = jnp.searchsorted(jnp.asarray(table, jnp.int32), pick, side="right")
    return jax.random.permutation(jax.random.fold_in(key, 2), number_of)[grade].astype(jnp.int32)


def noise(key, extent, scale, bound, split=(), kind=jnp.bfloat16):
    array = scale * jax.random.normal(key, extent, jnp.float32)
    if split:
        array = array * levels(key, extent, split, -0.22, 0.18)
    return jnp.clip(array, -bound, bound).astype(kind)


def setup_inputs(seed: int = 0) -> dict:
    arg_keys = jax.random.split(jax.random.key(seed), 9)
    centroids = jnp.clip(jax.random.uniform(arg_keys[0], (3, PANELS), jnp.float32, -4.0, 4.0) * levels(arg_keys[0], (3, PANELS), ((1, 512),), -0.4, 0.0), -4.0, 4.0)
    strengths = noise(arg_keys[1], (2 * NF, PANELS), 1.0, 6.0, ((1, 512),), jnp.float32)
    self_inv = noise(arg_keys[2], (2 * NF, PANELS), 1.0, 6.0, ((1, 512),), jnp.float32)
    wavenumbers = jnp.clip(jnp.exp(jax.random.uniform(arg_keys[3], (NF,), jnp.float32, math.log(0.3), math.log(2.0))), 0.3, 2.0)
    field_pos = jnp.clip(jax.random.uniform(arg_keys[4], (3, FIELD), jnp.float32, -4.0, 4.0) * levels(arg_keys[4], (3, FIELD), ((1, 32),), -0.4, 0.0), -4.0, 4.0)
    targets = noise(arg_keys[5], (2 * NF, FIELD), 1.0, 6.0, ((1, 32),), jnp.float32)
    lists = plant(ranked(arg_keys[6], (FIELD, LIST), PANELS, 2), jax.random.fold_in(arg_keys[6], 3), 0, PANELS - 1).astype(jnp.int32)
    connect = draw_connect(jax.random.fold_in(arg_keys[8], 71), 0)
    return {"centroids": centroids, "strengths": strengths, "self_inv": self_inv, "wavenumbers": wavenumbers, "field_pos": field_pos, "targets": targets, "lists": lists, "connect": connect}


SOFT = 1.0

def pair_block(target_pos, target_str, target_mu, source_pos, source_str, source_mu, wavenumbers):
    freqs = wavenumbers.shape[0]
    offset = target_pos[:, None, :] - source_pos[:, :, None]
    squared = lax.optimization_barrier(jnp.sum(offset * offset, axis=0)) + SOFT
    inverse = lax.rsqrt(squared)
    distance = squared * inverse
    inverse_sq = inverse * inverse
    phase = wavenumbers[:, None, None] * distance[None]
    cosine = jnp.cos(phase)
    sine = jnp.sin(phase)
    deriv_real = -(cosine + phase * sine) * inverse_sq
    deriv_imag = (phase * cosine - sine) * inverse_sq
    tgt_real = target_str[:freqs, None, :]
    tgt_imag = target_str[freqs:, None, :]
    tmu_real = target_mu[:freqs, None, :]
    tmu_imag = target_mu[freqs:, None, :]
    src_real = source_str[:freqs, :, None]
    src_imag = source_str[freqs:, :, None]
    smu_real = source_mu[:freqs, :, None]
    smu_imag = source_mu[freqs:, :, None]
    prod_real = tmu_real * src_real - tmu_imag * src_imag + smu_real * tgt_real - smu_imag * tgt_imag
    prod_imag = tmu_real * src_imag + tmu_imag * src_real + smu_real * tgt_imag + smu_imag * tgt_real
    weight = lax.optimization_barrier(jnp.sum(prod_real * deriv_real - prod_imag * deriv_imag, axis=0)) * inverse
    return lax.optimization_barrier(jnp.sum(weight[None] * offset, axis=1))

def reference(centroids, strengths, self_inv, wavenumbers, field_pos, targets, lists, connect):
    panel_ids = lists.reshape(-1)
    near = centroids[:, panel_ids]
    observer = jnp.repeat(field_pos, LIST, axis=1)
    offset = observer - near
    distance = jnp.sqrt(lax.optimization_barrier(jnp.sum(offset * offset, axis=0)) + SOFT)
    inverse = 1.0 / distance
    phase = wavenumbers[:, None] * distance[None]
    cosine = jnp.cos(phase)
    sine = jnp.sin(phase)
    str_real = strengths[:NF][:, panel_ids]
    str_imag = strengths[NF:][:, panel_ids]
    part_real = (cosine * str_real - sine * str_imag) * inverse
    part_imag = (cosine * str_imag + sine * str_real) * inverse
    eta_real = part_real.reshape(NF, FIELD, LIST).sum(axis=2)
    eta_imag = part_imag.reshape(NF, FIELD, LIST).sum(axis=2)
    res_real = eta_real - targets[:NF]
    res_imag = eta_imag - targets[NF:]
    objective = (jnp.sum(res_real * res_real) + jnp.sum(res_imag * res_imag)) / (NF * FIELD) + 1e-06
    rep_real = jnp.repeat(res_real, LIST, axis=1)
    rep_imag = jnp.repeat(res_imag, LIST, axis=1)
    term_real = (cosine * rep_real + sine * rep_imag) * inverse
    term_imag = (cosine * rep_imag - sine * rep_real) * inverse
    src_real = jnp.zeros((NF, PANELS), jnp.float32).at[:, panel_ids].add(term_real) / objective
    src_imag = jnp.zeros((NF, PANELS), jnp.float32).at[:, panel_ids].add(term_imag) / objective
    inv_real = self_inv[:NF]
    inv_imag = self_inv[NF:]
    adjoint = jnp.concatenate([src_real * inv_real - src_imag * inv_imag, src_real * inv_imag + src_imag * inv_real], axis=0)
    width = math.gcd(PANELS, 256)
    count = PANELS // width

    def one_target(start):
        tpos = lax.dynamic_slice_in_dim(centroids, start, width, 1)
        tstr = lax.dynamic_slice_in_dim(strengths, start, width, 1)
        tmu = lax.dynamic_slice_in_dim(adjoint, start, width, 1)

        def visit_block(total, sstart):
            spos = lax.dynamic_slice_in_dim(centroids, sstart, width, 1)
            sstr = lax.dynamic_slice_in_dim(strengths, sstart, width, 1)
            smu = lax.dynamic_slice_in_dim(adjoint, sstart, width, 1)
            return (total + pair_block(tpos, tstr, tmu, spos, sstr, smu, wavenumbers), None)
        total, _ = lax.scan(visit_block, jnp.zeros((3, width), jnp.float32), jnp.arange(count, dtype=jnp.int32) * width)
        return total
    blocks = lax.map(one_target, jnp.arange(count, dtype=jnp.int32) * width)
    panel_sens = jnp.transpose(blocks, (1, 0, 2)).reshape(3, PANELS) * (1.0 / math.sqrt(PANELS * NF))
    vertex_sens = jnp.zeros((3, VERTS), jnp.float32)
    for corner in range(4):
        vertex_sens = vertex_sens.at[:, connect[corner]].add(0.25 * panel_sens)
    return (adjoint, vertex_sens, objective)
```

```python
import math

import jax
import jax.numpy as jnp
from jax import lax
from jax.sharding import PartitionSpec as P

SOFT = 1.0


def pair_block(target_pos, target_str, target_mu, source_pos, source_str, source_mu, wavenumbers):
    freqs = wavenumbers.shape[0]
    offset = target_pos[:, None, :] - source_pos[:, :, None]
    squared = jnp.sum(offset * offset, axis=0) + SOFT
    inverse = lax.rsqrt(squared)
    distance = squared * inverse
    inverse_sq = inverse * inverse
    phase = wavenumbers[:, None, None] * distance[None]
    cosine = jnp.cos(phase)
    sine = jnp.sin(phase)
    deriv_real = -(cosine + phase * sine) * inverse_sq
    deriv_imag = (phase * cosine - sine) * inverse_sq
    tgt_real = target_str[:freqs, None, :]
    tgt_imag = target_str[freqs:, None, :]
    tmu_real = target_mu[:freqs, None, :]
    tmu_imag = target_mu[freqs:, None, :]
    src_real = source_str[:freqs, :, None]
    src_imag = source_str[freqs:, :, None]
    smu_real = source_mu[:freqs, :, None]
    smu_imag = source_mu[freqs:, :, None]
    prod_real = (
        tmu_real * src_real - tmu_imag * src_imag + smu_real * tgt_real - smu_imag * tgt_imag
    )
    prod_imag = (
        tmu_real * src_imag + tmu_imag * src_real + smu_real * tgt_imag + smu_imag * tgt_real
    )
    weight = jnp.sum(prod_real * deriv_real - prod_imag * deriv_imag, axis=0) * inverse
    return jnp.sum(weight[None] * offset, axis=1)


def pair_sweep(
    total, target_pos, target_str, target_mu, source_pos, source_str, source_mu, wavenumbers
):
    width = source_pos.shape[1]
    step = math.gcd(width, 128)

    def visit_block(carry, block_index):
        begin = block_index * step
        spos = lax.dynamic_slice_in_dim(source_pos, begin, step, 1)
        sstr = lax.dynamic_slice_in_dim(source_str, begin, step, 1)
        smu = lax.dynamic_slice_in_dim(source_mu, begin, step, 1)
        return (
            carry + pair_block(target_pos, target_str, target_mu, spos, sstr, smu, wavenumbers),
            None,
        )

    result, _ = lax.scan(visit_block, total, jnp.arange(width // step, dtype=jnp.int32))
    return result


def complex_times(left, right, freqs):
    left_real, left_imag = (left[:freqs], left[freqs:])
    right_real, right_imag = (right[:freqs], right[freqs:])
    return jnp.concatenate(
        [
            left_real * right_real - left_imag * right_imag,
            left_real * right_imag + left_imag * right_real,
        ],
        axis=0,
    )


def on_device(centroids, strengths, self_inv, wavenumbers, field_pos, targets, lists, connect):
    owned_count = centroids.shape[1]
    row_count = lax.axis_size("row")
    col_count = lax.axis_size("col")
    row_index = lax.axis_index("row")
    col_index = lax.axis_index("col")
    freqs = wavenumbers.shape[0]
    listed = lists.shape[1]
    panel_total = owned_count * row_count * col_count
    field_total = field_pos.shape[1] * row_count
    pos_rows = centroids.shape[0]
    str_rows = strengths.shape[0]
    owned = jnp.concatenate([centroids, strengths, self_inv], axis=0)
    src_all = lax.all_gather(owned, "row", axis=1, tiled=True)
    src_pos = src_all[:pos_rows]
    src_str = src_all[pos_rows : pos_rows + str_rows]
    src_inv = src_all[pos_rows + str_rows :]
    source_count = src_all.shape[1]
    panel_ids = lists.reshape(-1)
    owner_block = panel_ids // owned_count
    mask = (owner_block % col_count == col_index).astype(jnp.float32)
    local_ids = owner_block // col_count * owned_count + panel_ids % owned_count
    near_all = jnp.take(src_all[: pos_rows + str_rows], local_ids, axis=1)
    near = near_all[:pos_rows]
    observer = jnp.repeat(field_pos, listed, axis=1)
    offset = observer - near
    distance = jnp.sqrt(jnp.sum(offset * offset, axis=0) + SOFT)
    inverse = mask / distance
    phase = wavenumbers[:, None] * distance[None]
    cosine = jnp.cos(phase)
    sine = jnp.sin(phase)
    near_str = near_all[pos_rows:]
    str_real = near_str[:freqs]
    str_imag = near_str[freqs:]
    part_real = (cosine * str_real - sine * str_imag) * inverse
    part_imag = (cosine * str_imag + sine * str_real) * inverse
    eta_part = jnp.concatenate(
        [
            part_real.reshape(freqs, -1, listed).sum(axis=2),
            part_imag.reshape(freqs, -1, listed).sum(axis=2),
        ],
        axis=0,
    )
    eta = lax.psum(eta_part, "col")
    resid = eta - targets
    rep_real = jnp.repeat(resid[:freqs], listed, axis=1)
    rep_imag = jnp.repeat(resid[freqs:], listed, axis=1)
    term_real = (cosine * rep_real + sine * rep_imag) * inverse
    term_imag = (cosine * rep_imag - sine * rep_real) * inverse
    terms = jnp.concatenate([term_real, term_imag], axis=0)
    source_part = jnp.zeros((2 * freqs, source_count), jnp.float32).at[:, local_ids].add(terms)
    misfit_part = jnp.sum(resid * resid)
    misfit_row = jnp.where(
        lax.broadcasted_iota(jnp.int32, (1, source_count), 1) == 0, misfit_part, 0.0
    )
    packed = lax.psum(jnp.concatenate([source_part, misfit_row], axis=0), "row")
    objective = packed[2 * freqs, 0] / (freqs * field_total) + 1e-06
    source_all = packed[: 2 * freqs] / objective
    mu_all = complex_times(source_all, src_inv, freqs)
    mu_own = lax.dynamic_slice_in_dim(mu_all, row_index * owned_count, owned_count, 1)
    tgt_all = lax.all_gather(
        jnp.concatenate([centroids, strengths, mu_own], axis=0), "col", axis=1, tiled=True
    )
    tgt_pos = tgt_all[:pos_rows]
    tgt_str = tgt_all[pos_rows : pos_rows + str_rows]
    tgt_mu = tgt_all[pos_rows + str_rows :]
    block_width = tgt_pos.shape[1]
    empty = jnp.zeros((3, block_width), jnp.float32)
    accum = pair_sweep(empty, tgt_pos, tgt_str, tgt_mu, src_pos, src_str, mu_all, wavenumbers)
    panel_sens = accum * (1.0 / math.sqrt(panel_total * freqs))
    vertex_local = connect - row_index * block_width
    vertex_part = jnp.zeros((3, block_width), jnp.float32).at[:, vertex_local.reshape(-1)].add(
        jnp.tile(0.25 * panel_sens, (1, connect.shape[0]))
    )
    vertex_own = lax.psum_scatter(vertex_part, "col", scatter_dimension=1, tiled=True)
    adjoint = mu_own
    return (adjoint, vertex_own, objective)


def solution(mesh):
    return jax.shard_map(
        on_device,
        mesh=mesh,
        in_specs=(
            P(None, ("row", "col")),
            P(None, ("row", "col")),
            P(None, ("row", "col")),
            P(),
            P(None, "row"),
            P(None, "row"),
            P("row", None),
            P(None, "row"),
        ),
        out_specs=(P(None, ("row", "col")), P(None, ("row", "col")), P()),
        check_vma=False,
    )
```

```python
import math

import jax
import jax.numpy as jnp
from jax import lax
from jax.sharding import PartitionSpec as P

SOFT = 1.0


def pair_block(target_pos, target_str, target_mu, source_pos, source_str, source_mu, wavenumbers):
    freqs = wavenumbers.shape[0]
    offset = target_pos[:, None, :] - source_pos[:, :, None]
    squared = jnp.sum(offset * offset, axis=0) + SOFT
    inverse = lax.rsqrt(squared)
    distance = squared * inverse
    inverse_sq = inverse * inverse
    phase = wavenumbers[:, None, None] * distance[None]
    cosine = jnp.cos(phase)
    sine = jnp.sin(phase)
    deriv_real = -(cosine + phase * sine) * inverse_sq
    deriv_imag = (phase * cosine - sine) * inverse_sq
    tgt_real = target_str[:freqs, None, :]
    tgt_imag = target_str[freqs:, None, :]
    tmu_real = target_mu[:freqs, None, :]
    tmu_imag = target_mu[freqs:, None, :]
    src_real = source_str[:freqs, :, None]
    src_imag = source_str[freqs:, :, None]
    smu_real = source_mu[:freqs, :, None]
    smu_imag = source_mu[freqs:, :, None]
    prod_real = (
        tmu_real * src_real - tmu_imag * src_imag + smu_real * tgt_real - smu_imag * tgt_imag
    )
    prod_imag = (
        tmu_real * src_imag + tmu_imag * src_real + smu_real * tgt_imag + smu_imag * tgt_real
    )
    weight = jnp.sum(prod_real * deriv_real - prod_imag * deriv_imag, axis=0) * inverse
    return jnp.sum(weight[None] * offset, axis=1)


def pair_sweep(
    total, target_pos, target_str, target_mu, source_pos, source_str, source_mu, wavenumbers
):
    width = source_pos.shape[1]
    step = math.gcd(width, 128)

    def visit_block(carry, block_index):
        begin = block_index * step
        spos = lax.dynamic_slice_in_dim(source_pos, begin, step, 1)
        sstr = lax.dynamic_slice_in_dim(source_str, begin, step, 1)
        smu = lax.dynamic_slice_in_dim(source_mu, begin, step, 1)
        return (
            carry + pair_block(target_pos, target_str, target_mu, spos, sstr, smu, wavenumbers),
            None,
        )

    result, _ = lax.scan(visit_block, total, jnp.arange(width // step, dtype=jnp.int32))
    return result


def complex_times(left, right, freqs):
    left_real, left_imag = (left[:freqs], left[freqs:])
    right_real, right_imag = (right[:freqs], right[freqs:])
    return jnp.concatenate(
        [
            left_real * right_real - left_imag * right_imag,
            left_real * right_imag + left_imag * right_real,
        ],
        axis=0,
    )


def xor_psum(value, axis):
    count = lax.axis_size(axis)
    shift = 1
    while shift < count:
        partner = [(index, index ^ shift) for index in range(count)]
        value = value + lax.ppermute(value, axis, partner)
        shift *= 2
    return value


def on_device(centroids, strengths, self_inv, wavenumbers, field_pos, targets, lists, connect):
    owned_count = centroids.shape[1]
    row_count = lax.axis_size("row")
    col_count = lax.axis_size("col")
    row_index = lax.axis_index("row")
    col_index = lax.axis_index("col")
    freqs = wavenumbers.shape[0]
    listed = lists.shape[1]
    panel_total = owned_count * row_count * col_count
    field_total = field_pos.shape[1] * row_count
    pos_rows = centroids.shape[0]
    str_rows = strengths.shape[0]
    owned = jnp.concatenate([centroids, strengths, self_inv], axis=0)
    src_all = lax.all_gather(owned, "row", axis=1, tiled=True)
    src_pos = src_all[:pos_rows]
    src_str = src_all[pos_rows : pos_rows + str_rows]
    src_inv = src_all[pos_rows + str_rows :]
    source_count = src_all.shape[1]
    panel_ids = lists.reshape(-1)
    owner_block = panel_ids // owned_count
    mask = (owner_block % col_count == col_index).astype(jnp.float32)
    local_ids = owner_block // col_count * owned_count + panel_ids % owned_count
    near_all = jnp.take(src_all[: pos_rows + str_rows], local_ids, axis=1)
    near = near_all[:pos_rows]
    observer = jnp.repeat(field_pos, listed, axis=1)
    offset = observer - near
    distance = jnp.sqrt(jnp.sum(offset * offset, axis=0) + SOFT)
    inverse = mask / distance
    phase = wavenumbers[:, None] * distance[None]
    cosine = jnp.cos(phase)
    sine = jnp.sin(phase)
    near_str = near_all[pos_rows:]
    str_real = near_str[:freqs]
    str_imag = near_str[freqs:]
    part_real = (cosine * str_real - sine * str_imag) * inverse
    part_imag = (cosine * str_imag + sine * str_real) * inverse
    eta_part = jnp.concatenate(
        [
            part_real.reshape(freqs, -1, listed).sum(axis=2),
            part_imag.reshape(freqs, -1, listed).sum(axis=2),
        ],
        axis=0,
    )
    eta = xor_psum(eta_part, "col")
    resid = eta - targets
    rep_real = jnp.repeat(resid[:freqs], listed, axis=1)
    rep_imag = jnp.repeat(resid[freqs:], listed, axis=1)
    term_real = (cosine * rep_real + sine * rep_imag) * inverse
    term_imag = (cosine * rep_imag - sine * rep_real) * inverse
    terms = jnp.concatenate([term_real, term_imag], axis=0)
    source_part = jnp.zeros((2 * freqs, source_count), jnp.float32).at[:, local_ids].add(terms)
    misfit_part = jnp.sum(resid * resid)
    misfit_row = jnp.where(
        lax.broadcasted_iota(jnp.int32, (1, source_count), 1) == 0, misfit_part, 0.0
    )
    packed = xor_psum(jnp.concatenate([source_part, misfit_row], axis=0), "row")
    objective = packed[2 * freqs, 0] / (freqs * field_total) + 1e-06
    source_all = packed[: 2 * freqs] / objective
    mu_all = complex_times(source_all, src_inv, freqs)
    mu_own = lax.dynamic_slice_in_dim(mu_all, row_index * owned_count, owned_count, 1)
    tgt_all = lax.all_gather(
        jnp.concatenate([centroids, strengths, mu_own], axis=0), "col", axis=1, tiled=True
    )
    tgt_pos = tgt_all[:pos_rows]
    tgt_str = tgt_all[pos_rows : pos_rows + str_rows]
    tgt_mu = tgt_all[pos_rows + str_rows :]
    block_width = tgt_pos.shape[1]
    empty = jnp.zeros((3, block_width), jnp.float32)
    accum = pair_sweep(empty, tgt_pos, tgt_str, tgt_mu, src_pos, src_str, mu_all, wavenumbers)
    panel_sens = accum * (1.0 / math.sqrt(panel_total * freqs))
    vertex_local = connect - row_index * block_width
    vertex_part = jnp.zeros((3, block_width), jnp.float32).at[:, vertex_local.reshape(-1)].add(
        jnp.tile(0.25 * panel_sens, (1, connect.shape[0]))
    )
    vertex_own = lax.dynamic_slice_in_dim(
        xor_psum(vertex_part, "col"), col_index * owned_count, owned_count, 1
    )
    adjoint = mu_own
    return (adjoint, vertex_own, objective)


def solution(mesh):
    return jax.shard_map(
        on_device,
        mesh=mesh,
        in_specs=(
            P(None, ("row", "col")),
            P(None, ("row", "col")),
            P(None, ("row", "col")),
            P(),
            P(None, "row"),
            P(None, "row"),
            P("row", None),
            P(None, "row"),
        ),
        out_specs=(P(None, ("row", "col")), P(None, ("row", "col")), P()),
        check_vma=False,
    )
```

```python
import math

import jax
import jax.numpy as jnp
from jax import lax
from jax.experimental.layout import Layout, with_layout_constraint
from jax.sharding import PartitionSpec as P

SOFT = 1.0


def pair_block(target_pos, target_str, target_mu, source_pos, source_str, source_mu, wavenumbers):
    freqs = wavenumbers.shape[0]
    offset = target_pos[:, None, :] - source_pos[:, :, None]
    squared = jnp.sum(offset * offset, axis=0) + SOFT
    inverse = lax.rsqrt(squared)
    distance = squared * inverse
    inverse_sq = inverse * inverse
    phase = wavenumbers[:, None, None] * distance[None]
    cosine = jnp.cos(phase)
    sine = jnp.sin(phase)
    deriv_real = -(cosine + phase * sine) * inverse_sq
    deriv_imag = (phase * cosine - sine) * inverse_sq
    tgt_real = target_str[:freqs, None, :]
    tgt_imag = target_str[freqs:, None, :]
    tmu_real = target_mu[:freqs, None, :]
    tmu_imag = target_mu[freqs:, None, :]
    src_real = source_str[:freqs, :, None]
    src_imag = source_str[freqs:, :, None]
    smu_real = source_mu[:freqs, :, None]
    smu_imag = source_mu[freqs:, :, None]
    prod_real = (
        tmu_real * src_real - tmu_imag * src_imag + smu_real * tgt_real - smu_imag * tgt_imag
    )
    prod_imag = (
        tmu_real * src_imag + tmu_imag * src_real + smu_real * tgt_imag + smu_imag * tgt_real
    )
    weight = jnp.sum(prod_real * deriv_real - prod_imag * deriv_imag, axis=0) * inverse
    return jnp.sum(weight[None] * offset, axis=1)


def pair_sweep(
    total, target_pos, target_str, target_mu, source_pos, source_str, source_mu, wavenumbers
):
    width = source_pos.shape[1]
    step = math.gcd(width, 128)

    def visit_block(carry, block_index):
        begin = block_index * step
        spos = lax.dynamic_slice_in_dim(source_pos, begin, step, 1)
        sstr = lax.dynamic_slice_in_dim(source_str, begin, step, 1)
        smu = lax.dynamic_slice_in_dim(source_mu, begin, step, 1)
        return (
            carry + pair_block(target_pos, target_str, target_mu, spos, sstr, smu, wavenumbers),
            None,
        )

    result, _ = lax.scan(visit_block, total, jnp.arange(width // step, dtype=jnp.int32))
    return result


def complex_times(left, right, freqs):
    left_real, left_imag = (left[:freqs], left[freqs:])
    right_real, right_imag = (right[:freqs], right[freqs:])
    return jnp.concatenate(
        [
            left_real * right_real - left_imag * right_imag,
            left_real * right_imag + left_imag * right_real,
        ],
        axis=0,
    )


def row_major(value):
    return with_layout_constraint(value, Layout(tuple(range(value.ndim))))


def xor_psum(value, axis):
    count = lax.axis_size(axis)
    shift = 1
    while shift < count:
        partner = [(index, index ^ shift) for index in range(count)]
        value = row_major(value)
        value = value + lax.ppermute(value, axis, partner)
        shift *= 2
    return value


def halving_scatter(value, axis):
    count = lax.axis_size(axis)
    me = lax.axis_index(axis)
    shift = 1
    while shift < count:
        half = value.shape[1] // 2
        low, high = value[:, :half], value[:, half:]
        upper = (me // shift) % 2 == 1
        keep = jnp.where(upper, high, low)
        send = row_major(jnp.where(upper, low, high))
        partner = [(index, index ^ shift) for index in range(count)]
        value = keep + lax.ppermute(send, axis, partner)
        shift *= 2
    return value


def bit_reverse(value, bits):
    result = jnp.zeros_like(value)
    for bit in range(bits):
        result = result | (((value >> bit) & 1) << (bits - 1 - bit))
    return result


def on_device(centroids, strengths, self_inv, wavenumbers, field_pos, targets, lists, connect):
    owned_count = centroids.shape[1]
    row_count = lax.axis_size("row")
    col_count = lax.axis_size("col")
    row_index = lax.axis_index("row")
    col_index = lax.axis_index("col")
    freqs = wavenumbers.shape[0]
    listed = lists.shape[1]
    panel_total = owned_count * row_count * col_count
    field_total = field_pos.shape[1] * row_count
    pos_rows = centroids.shape[0]
    str_rows = strengths.shape[0]
    owned = jnp.concatenate([centroids, strengths, self_inv], axis=0)
    src_all = lax.all_gather(owned, "row", axis=1, tiled=True)
    src_pos = src_all[:pos_rows]
    src_str = src_all[pos_rows : pos_rows + str_rows]
    src_inv = src_all[pos_rows + str_rows :]
    source_count = src_all.shape[1]
    panel_ids = lists.reshape(-1)
    owner_block = panel_ids // owned_count
    owner_row = owner_block // col_count
    mask = (owner_block % col_count == col_index).astype(jnp.float32)
    local_ids = owner_row * owned_count + panel_ids % owned_count
    table = jnp.transpose(src_all[: pos_rows + str_rows])
    near_all = jnp.transpose(jnp.take(table, local_ids, axis=0))
    near = near_all[:pos_rows]
    observer = jnp.repeat(field_pos, listed, axis=1)
    offset = observer - near
    distance = jnp.sqrt(jnp.sum(offset * offset, axis=0) + SOFT)
    inverse = mask / distance
    phase = wavenumbers[:, None] * distance[None]
    cosine = jnp.cos(phase)
    sine = jnp.sin(phase)
    near_str = near_all[pos_rows:]
    str_real = near_str[:freqs]
    str_imag = near_str[freqs:]
    part_real = (cosine * str_real - sine * str_imag) * inverse
    part_imag = (cosine * str_imag + sine * str_real) * inverse
    eta_part = jnp.concatenate(
        [
            part_real.reshape(freqs, -1, listed).sum(axis=2),
            part_imag.reshape(freqs, -1, listed).sum(axis=2),
        ],
        axis=0,
    )
    eta = xor_psum(eta_part, "col")
    resid = eta - targets
    rep_real = jnp.repeat(resid[:freqs], listed, axis=1)
    rep_imag = jnp.repeat(resid[freqs:], listed, axis=1)
    term_real = (cosine * rep_real + sine * rep_imag) * inverse
    term_imag = (cosine * rep_imag - sine * rep_real) * inverse
    terms = jnp.concatenate([term_real, term_imag], axis=0)
    row_bits = max(row_count - 1, 0).bit_length()
    slot_ids = bit_reverse(owner_row, row_bits) * owned_count + panel_ids % owned_count
    source_part = jnp.zeros((source_count, 2 * freqs), jnp.float32).at[slot_ids].add(
        jnp.transpose(terms)
    )
    misfit_part = jnp.sum(resid * resid)
    misfit_row = jnp.full((1, source_count), misfit_part, jnp.float32)
    packed = halving_scatter(
        jnp.concatenate([jnp.transpose(source_part), misfit_row], axis=0), "row"
    )
    objective = packed[2 * freqs, 0] / (freqs * field_total) + 1e-06
    source_own = packed[: 2 * freqs] / objective
    mu_own = complex_times(source_own, self_inv, freqs)
    mu_all = lax.all_gather(mu_own, "row", axis=1, tiled=True)
    tgt_all = lax.all_gather(
        jnp.concatenate([centroids, strengths, mu_own], axis=0), "col", axis=1, tiled=True
    )
    tgt_pos = tgt_all[:pos_rows]
    tgt_str = tgt_all[pos_rows : pos_rows + str_rows]
    tgt_mu = tgt_all[pos_rows + str_rows :]
    block_width = tgt_pos.shape[1]
    empty = jnp.zeros((3, block_width), jnp.float32)
    accum = pair_sweep(empty, tgt_pos, tgt_str, tgt_mu, src_pos, src_str, mu_all, wavenumbers)
    panel_sens = accum * (1.0 / math.sqrt(panel_total * freqs))
    vertex_local = connect - row_index * block_width
    vertex_part = jnp.zeros((3, block_width), jnp.float32).at[:, vertex_local.reshape(-1)].add(
        jnp.tile(0.25 * panel_sens, (1, connect.shape[0]))
    )
    lanes = 128 if block_width % 128 == 0 else block_width
    vertex_rows = vertex_part.reshape(3 * block_width // lanes, lanes)
    vertex_sum = xor_psum(vertex_rows, "col").reshape(3, block_width)
    vertex_own = lax.dynamic_slice_in_dim(vertex_sum, col_index * owned_count, owned_count, 1)
    adjoint = mu_own
    return (adjoint, vertex_own, objective)


def solution(mesh):
    return jax.shard_map(
        on_device,
        mesh=mesh,
        in_specs=(
            P(None, ("row", "col")),
            P(None, ("row", "col")),
            P(None, ("row", "col")),
            P(),
            P(None, "row"),
            P(None, "row"),
            P("row", None),
            P(None, "row"),
        ),
        out_specs=(P(None, ("row", "col")), P(None, ("row", "col")), P()),
        check_vma=False,
    )
```

```python
import math

import jax
import jax.numpy as jnp
from jax import lax
from jax.experimental.layout import Layout, with_layout_constraint
from jax.sharding import PartitionSpec as P

SOFT = 1.0


def sincos(angle):
    quarter = jnp.round(angle * (2.0 / math.pi))
    rest = angle - quarter * 1.5703125
    rest = rest - quarter * 4.837512969970703125e-4
    rest = rest - quarter * 7.54978995489188216e-8
    rest_sq = rest * rest
    odd = rest + rest * rest_sq * (
        -1.6666654611e-1 + rest_sq * (8.3321608736e-3 + rest_sq * -1.9515295891e-4)
    )
    even = (
        1.0
        - 0.5 * rest_sq
        + rest_sq
        * rest_sq
        * (4.166664568298827e-2 + rest_sq * (-1.388731625493765e-3 + rest_sq * 2.443315711809948e-5))
    )
    turn = quarter.astype(jnp.int32)
    swap = (turn & 1) == 1
    sine = jnp.where(swap, even, odd)
    cosine = jnp.where(swap, odd, even)
    sine = jnp.where((turn & 2) == 2, -sine, sine)
    cosine = jnp.where(((turn + 1) & 2) == 2, -cosine, cosine)
    return sine, cosine


def pair_block(target_pos, target_str, target_mu, source_pos, source_str, source_mu, wavenumbers):
    freqs = wavenumbers.shape[0]
    offset = target_pos[:, None, :] - source_pos[:, :, None]
    squared = jnp.sum(offset * offset, axis=0) + SOFT
    inverse = lax.rsqrt(squared)
    distance = squared * inverse
    phase = wavenumbers[:, None, None] * distance[None]
    sine, cosine = sincos(phase)
    tgt_real = target_str[:freqs, None, :]
    tgt_imag = target_str[freqs:, None, :]
    tmu_real = target_mu[:freqs, None, :]
    tmu_imag = target_mu[freqs:, None, :]
    src_real = source_str[:freqs, :, None]
    src_imag = source_str[freqs:, :, None]
    smu_real = source_mu[:freqs, :, None]
    smu_imag = source_mu[freqs:, :, None]
    prod_real = (
        tmu_real * src_real - tmu_imag * src_imag + smu_real * tgt_real - smu_imag * tgt_imag
    )
    prod_imag = (
        tmu_real * src_imag + tmu_imag * src_real + smu_real * tgt_imag + smu_imag * tgt_real
    )
    inner = cosine * (prod_real + phase * prod_imag) + sine * (phase * prod_real - prod_imag)
    weight = -jnp.sum(inner, axis=0) * (inverse * inverse * inverse)
    return jnp.sum(weight[None] * offset, axis=1)


def pair_sweep(
    total, target_pos, target_str, target_mu, source_pos, source_str, source_mu, wavenumbers
):
    width = source_pos.shape[1]
    step = math.gcd(width, 128)

    def visit_block(carry, block_index):
        begin = block_index * step
        spos = lax.dynamic_slice_in_dim(source_pos, begin, step, 1)
        sstr = lax.dynamic_slice_in_dim(source_str, begin, step, 1)
        smu = lax.dynamic_slice_in_dim(source_mu, begin, step, 1)
        return (
            carry + pair_block(target_pos, target_str, target_mu, spos, sstr, smu, wavenumbers),
            None,
        )

    result, _ = lax.scan(visit_block, total, jnp.arange(width // step, dtype=jnp.int32))
    return result


def complex_times(left, right, freqs):
    left_real, left_imag = (left[:freqs], left[freqs:])
    right_real, right_imag = (right[:freqs], right[freqs:])
    return jnp.concatenate(
        [
            left_real * right_real - left_imag * right_imag,
            left_real * right_imag + left_imag * right_real,
        ],
        axis=0,
    )


def row_major(value):
    return with_layout_constraint(value, Layout(tuple(range(value.ndim))))


def xor_psum(value, axis):
    count = lax.axis_size(axis)
    shift = 1
    while shift < count:
        partner = [(index, index ^ shift) for index in range(count)]
        value = row_major(value)
        value = value + lax.ppermute(value, axis, partner)
        shift *= 2
    return value


def halving_scatter(value, axis):
    count = lax.axis_size(axis)
    me = lax.axis_index(axis)
    shift = 1
    while shift < count:
        half = value.shape[1] // 2
        low, high = value[:, :half], value[:, half:]
        upper = (me // shift) % 2 == 1
        keep = jnp.where(upper, high, low)
        send = row_major(jnp.where(upper, low, high))
        partner = [(index, index ^ shift) for index in range(count)]
        value = keep + lax.ppermute(send, axis, partner)
        shift *= 2
    return value


def bit_reverse(value, bits):
    result = jnp.zeros_like(value)
    for bit in range(bits):
        result = result | (((value >> bit) & 1) << (bits - 1 - bit))
    return result


def on_device(centroids, strengths, self_inv, wavenumbers, field_pos, targets, lists, connect):
    owned_count = centroids.shape[1]
    row_count = lax.axis_size("row")
    col_count = lax.axis_size("col")
    row_index = lax.axis_index("row")
    col_index = lax.axis_index("col")
    freqs = wavenumbers.shape[0]
    listed = lists.shape[1]
    panel_total = owned_count * row_count * col_count
    field_total = field_pos.shape[1] * row_count
    pos_rows = centroids.shape[0]
    str_rows = strengths.shape[0]
    owned = jnp.concatenate([centroids, strengths, self_inv], axis=0)
    src_all = lax.all_gather(owned, "row", axis=1, tiled=True)
    src_pos = src_all[:pos_rows]
    src_str = src_all[pos_rows : pos_rows + str_rows]
    src_inv = src_all[pos_rows + str_rows :]
    source_count = src_all.shape[1]
    panel_ids = lists.reshape(-1)
    owner_block = panel_ids // owned_count
    owner_row = owner_block // col_count
    mask = (owner_block % col_count == col_index).astype(jnp.float32)
    local_ids = owner_row * owned_count + panel_ids % owned_count
    table = jnp.transpose(src_all[: pos_rows + str_rows])
    near_all = jnp.transpose(jnp.take(table, local_ids, axis=0))
    near = near_all[:pos_rows]
    observer = jnp.repeat(field_pos, listed, axis=1)
    offset = observer - near
    distance = jnp.sqrt(jnp.sum(offset * offset, axis=0) + SOFT)
    inverse = mask / distance
    phase = wavenumbers[:, None] * distance[None]
    sine, cosine = sincos(phase)
    near_str = near_all[pos_rows:]
    str_real = near_str[:freqs]
    str_imag = near_str[freqs:]
    part_real = (cosine * str_real - sine * str_imag) * inverse
    part_imag = (cosine * str_imag + sine * str_real) * inverse
    eta_part = jnp.concatenate(
        [
            part_real.reshape(freqs, -1, listed).sum(axis=2),
            part_imag.reshape(freqs, -1, listed).sum(axis=2),
        ],
        axis=0,
    )
    eta = xor_psum(eta_part, "col")
    resid = eta - targets
    rep_real = jnp.repeat(resid[:freqs], listed, axis=1)
    rep_imag = jnp.repeat(resid[freqs:], listed, axis=1)
    term_real = (cosine * rep_real + sine * rep_imag) * inverse
    term_imag = (cosine * rep_imag - sine * rep_real) * inverse
    terms = jnp.concatenate([term_real, term_imag], axis=0)
    row_bits = max(row_count - 1, 0).bit_length()
    slot_ids = bit_reverse(owner_row, row_bits) * owned_count + panel_ids % owned_count
    source_part = jnp.zeros((source_count, 2 * freqs), jnp.float32).at[slot_ids].add(
        jnp.transpose(terms)
    )
    misfit_part = jnp.sum(resid * resid)
    misfit_row = jnp.full((1, source_count), misfit_part, jnp.float32)
    packed = halving_scatter(
        jnp.concatenate([jnp.transpose(source_part), misfit_row], axis=0), "row"
    )
    objective = packed[2 * freqs, 0] / (freqs * field_total) + 1e-06
    source_own = packed[: 2 * freqs] / objective
    mu_own = complex_times(source_own, self_inv, freqs)
    mu_all = lax.all_gather(mu_own, "row", axis=1, tiled=True)
    tgt_all = lax.all_gather(
        jnp.concatenate([centroids, strengths, mu_own], axis=0), "col", axis=1, tiled=True
    )
    tgt_pos = tgt_all[:pos_rows]
    tgt_str = tgt_all[pos_rows : pos_rows + str_rows]
    tgt_mu = tgt_all[pos_rows + str_rows :]
    block_width = tgt_pos.shape[1]
    empty = jnp.zeros((3, block_width), jnp.float32)
    accum = pair_sweep(empty, tgt_pos, tgt_str, tgt_mu, src_pos, src_str, mu_all, wavenumbers)
    panel_sens = accum * (1.0 / math.sqrt(panel_total * freqs))
    vertex_local = connect - row_index * block_width
    vertex_part = jnp.zeros((3, block_width), jnp.float32).at[:, vertex_local.reshape(-1)].add(
        jnp.tile(0.25 * panel_sens, (1, connect.shape[0]))
    )
    lanes = 128 if block_width % 128 == 0 else block_width
    vertex_rows = vertex_part.reshape(3 * block_width // lanes, lanes)
    vertex_sum = xor_psum(vertex_rows, "col").reshape(3, block_width)
    vertex_own = lax.dynamic_slice_in_dim(vertex_sum, col_index * owned_count, owned_count, 1)
    adjoint = mu_own
    return (adjoint, vertex_own, objective)


def solution(mesh):
    return jax.shard_map(
        on_device,
        mesh=mesh,
        in_specs=(
            P(None, ("row", "col")),
            P(None, ("row", "col")),
            P(None, ("row", "col")),
            P(),
            P(None, "row"),
            P(None, "row"),
            P("row", None),
            P(None, "row"),
        ),
        out_specs=(P(None, ("row", "col")), P(None, ("row", "col")), P()),
        check_vma=False,
    )
```

```python
import math

import jax
import jax.numpy as jnp
from jax import lax
from jax.experimental.layout import Layout, with_layout_constraint
from jax.sharding import PartitionSpec as P

SOFT = 1.0


def sincos(angle):
    quarter = jnp.round(angle * (2.0 / math.pi))
    rest = angle - quarter * 1.5703125
    rest = rest - quarter * 4.837512969970703125e-4
    rest = rest - quarter * 7.54978995489188216e-8
    rest_sq = rest * rest
    odd = rest + rest * rest_sq * (
        -1.6666654611e-1 + rest_sq * (8.3321608736e-3 + rest_sq * -1.9515295891e-4)
    )
    even = (
        1.0
        - 0.5 * rest_sq
        + rest_sq
        * rest_sq
        * (4.166664568298827e-2 + rest_sq * (-1.388731625493765e-3 + rest_sq * 2.443315711809948e-5))
    )
    turn = quarter.astype(jnp.int32)
    swap = (turn & 1) == 1
    sine = jnp.where(swap, even, odd)
    cosine = jnp.where(swap, odd, even)
    sine = jnp.where((turn & 2) == 2, -sine, sine)
    cosine = jnp.where(((turn + 1) & 2) == 2, -cosine, cosine)
    return sine, cosine


def pair_block(target_pos, target_str, target_mu, source_pos, source_str, source_mu, wavenumbers):
    freqs = wavenumbers.shape[0]
    offset = target_pos[:, None, :] - source_pos[:, :, None]
    squared = jnp.sum(offset * offset, axis=0) + SOFT
    inverse = lax.rsqrt(squared)
    distance = squared * inverse
    phase = wavenumbers[:, None, None] * distance[None]
    sine, cosine = sincos(phase)
    tgt_real = target_str[:freqs, None, :]
    tgt_imag = target_str[freqs:, None, :]
    tmu_real = target_mu[:freqs, None, :]
    tmu_imag = target_mu[freqs:, None, :]
    src_real = source_str[:freqs, :, None]
    src_imag = source_str[freqs:, :, None]
    smu_real = source_mu[:freqs, :, None]
    smu_imag = source_mu[freqs:, :, None]
    prod_real = (
        tmu_real * src_real - tmu_imag * src_imag + smu_real * tgt_real - smu_imag * tgt_imag
    )
    prod_imag = (
        tmu_real * src_imag + tmu_imag * src_real + smu_real * tgt_imag + smu_imag * tgt_real
    )
    inner = cosine * (prod_real + phase * prod_imag) + sine * (phase * prod_real - prod_imag)
    weight = -jnp.sum(inner, axis=0) * (inverse * inverse * inverse)
    return jnp.sum(weight[None] * offset, axis=1)


def pair_sweep(
    total, target_pos, target_str, target_mu, source_pos, source_str, source_mu, wavenumbers
):
    width = source_pos.shape[1]
    step = math.gcd(width, 256)

    def visit_block(carry, block_index):
        begin = block_index * step
        spos = lax.dynamic_slice_in_dim(source_pos, begin, step, 1)
        sstr = lax.dynamic_slice_in_dim(source_str, begin, step, 1)
        smu = lax.dynamic_slice_in_dim(source_mu, begin, step, 1)
        return (
            carry + pair_block(target_pos, target_str, target_mu, spos, sstr, smu, wavenumbers),
            None,
        )

    result, _ = lax.scan(visit_block, total, jnp.arange(width // step, dtype=jnp.int32))
    return result


def complex_times(left, right, freqs):
    left_real, left_imag = (left[:freqs], left[freqs:])
    right_real, right_imag = (right[:freqs], right[freqs:])
    return jnp.concatenate(
        [
            left_real * right_real - left_imag * right_imag,
            left_real * right_imag + left_imag * right_real,
        ],
        axis=0,
    )


def row_major(value):
    return with_layout_constraint(value, Layout(tuple(range(value.ndim))))


def xor_psum(value, axis):
    count = lax.axis_size(axis)
    shift = 1
    while shift < count:
        partner = [(index, index ^ shift) for index in range(count)]
        value = row_major(value)
        value = value + lax.ppermute(value, axis, partner)
        shift *= 2
    return value


def halving_scatter(value, axis):
    count = lax.axis_size(axis)
    me = lax.axis_index(axis)
    shift = 1
    while shift < count:
        half = value.shape[1] // 2
        low, high = value[:, :half], value[:, half:]
        upper = (me // shift) % 2 == 1
        keep = jnp.where(upper, high, low)
        send = row_major(jnp.where(upper, low, high))
        partner = [(index, index ^ shift) for index in range(count)]
        value = keep + lax.ppermute(send, axis, partner)
        shift *= 2
    return value


def bit_reverse(value, bits):
    result = jnp.zeros_like(value)
    for bit in range(bits):
        result = result | (((value >> bit) & 1) << (bits - 1 - bit))
    return result


def split_three(value):
    high = lax.reduce_precision(value, exponent_bits=8, mantissa_bits=7)
    rest = value - high
    middle = lax.reduce_precision(rest, exponent_bits=8, mantissa_bits=7)
    low = rest - middle
    return jnp.concatenate([high, middle, low], axis=0).astype(jnp.bfloat16)


def join_three(value):
    rows = value.shape[0] // 3
    return (value[:rows] + value[rows : 2 * rows]) + value[2 * rows :]


def on_device(centroids, strengths, self_inv, wavenumbers, field_pos, targets, lists, connect):
    owned_count = centroids.shape[1]
    row_count = lax.axis_size("row")
    col_count = lax.axis_size("col")
    row_index = lax.axis_index("row")
    col_index = lax.axis_index("col")
    freqs = wavenumbers.shape[0]
    listed = lists.shape[1]
    panel_total = owned_count * row_count * col_count
    field_total = field_pos.shape[1] * row_count
    pos_rows = centroids.shape[0]
    str_rows = strengths.shape[0]
    owned = jnp.concatenate([centroids, strengths, self_inv], axis=0)
    src_all = lax.all_gather(owned, "row", axis=1, tiled=True)
    src_pos = src_all[:pos_rows]
    src_str = src_all[pos_rows : pos_rows + str_rows]
    src_inv = src_all[pos_rows + str_rows :]
    source_count = src_all.shape[1]
    panel_ids = lists.reshape(-1)
    owner_block = panel_ids // owned_count
    owner_row = owner_block // col_count
    mask = (owner_block % col_count == col_index).astype(jnp.float32)
    row_bits = max(row_count - 1, 0).bit_length()
    slot_ids = bit_reverse(owner_row, row_bits) * owned_count + panel_ids % owned_count
    slot_order = [
        sum(((slot >> bit) & 1) << (row_bits - 1 - bit) for bit in range(row_bits))
        for slot in range(row_count)
    ]
    table = src_all[: pos_rows + str_rows].reshape(-1, row_count, owned_count)
    table = jnp.concatenate([table[:, slot] for slot in slot_order], axis=1)
    onehot = (
        slot_ids[None, :] == lax.broadcasted_iota(jnp.int32, (source_count, slot_ids.shape[0]), 0)
    ).astype(jnp.bfloat16)
    near_all = join_three(
        jnp.dot(split_three(table), onehot, preferred_element_type=jnp.float32)
    )
    near = near_all[:pos_rows]
    observer = jnp.repeat(field_pos, listed, axis=1)
    offset = observer - near
    distance = jnp.sqrt(jnp.sum(offset * offset, axis=0) + SOFT)
    inverse = mask / distance
    phase = wavenumbers[:, None] * distance[None]
    sine, cosine = sincos(phase)
    near_str = near_all[pos_rows:]
    str_real = near_str[:freqs]
    str_imag = near_str[freqs:]
    part_real = (cosine * str_real - sine * str_imag) * inverse
    part_imag = (cosine * str_imag + sine * str_real) * inverse
    eta_part = jnp.concatenate(
        [
            part_real.reshape(freqs, -1, listed).sum(axis=2),
            part_imag.reshape(freqs, -1, listed).sum(axis=2),
        ],
        axis=0,
    )
    eta = xor_psum(eta_part, "col")
    resid = eta - targets
    rep_real = jnp.repeat(resid[:freqs], listed, axis=1)
    rep_imag = jnp.repeat(resid[freqs:], listed, axis=1)
    term_real = (cosine * rep_real + sine * rep_imag) * inverse
    term_imag = (cosine * rep_imag - sine * rep_real) * inverse
    terms = jnp.concatenate([term_real, term_imag], axis=0)
    source_part = join_three(
        lax.dot_general(
            split_three(terms),
            onehot,
            (((1,), (1,)), ((), ())),
            preferred_element_type=jnp.float32,
        )
    )
    misfit_part = jnp.sum(resid * resid)
    misfit_row = jnp.full((1, source_count), misfit_part, jnp.float32)
    packed = halving_scatter(
        jnp.concatenate([source_part, misfit_row], axis=0), "row"
    )
    objective = packed[2 * freqs, 0] / (freqs * field_total) + 1e-06
    source_own = packed[: 2 * freqs] / objective
    mu_own = complex_times(source_own, self_inv, freqs)
    mu_all = lax.all_gather(mu_own, "row", axis=1, tiled=True)
    tgt_all = lax.all_gather(
        jnp.concatenate([centroids, strengths, mu_own], axis=0), "col", axis=1, tiled=True
    )
    tgt_pos = tgt_all[:pos_rows]
    tgt_str = tgt_all[pos_rows : pos_rows + str_rows]
    tgt_mu = tgt_all[pos_rows + str_rows :]
    block_width = tgt_pos.shape[1]
    empty = jnp.zeros((3, block_width), jnp.float32)
    accum = pair_sweep(empty, tgt_pos, tgt_str, tgt_mu, src_pos, src_str, mu_all, wavenumbers)
    panel_sens = accum * (1.0 / math.sqrt(panel_total * freqs))
    vertex_local = connect - row_index * block_width
    vertex_part = jnp.zeros((3, block_width), jnp.float32).at[:, vertex_local.reshape(-1)].add(
        jnp.tile(0.25 * panel_sens, (1, connect.shape[0]))
    )
    lanes = 128 if block_width % 128 == 0 else block_width
    vertex_rows = vertex_part.reshape(3 * block_width // lanes, lanes)
    vertex_sum = xor_psum(vertex_rows, "col").reshape(3, block_width)
    vertex_own = lax.dynamic_slice_in_dim(vertex_sum, col_index * owned_count, owned_count, 1)
    adjoint = mu_own
    return (adjoint, vertex_own, objective)


def solution(mesh):
    return jax.shard_map(
        on_device,
        mesh=mesh,
        in_specs=(
            P(None, ("row", "col")),
            P(None, ("row", "col")),
            P(None, ("row", "col")),
            P(),
            P(None, "row"),
            P(None, "row"),
            P("row", None),
            P(None, "row"),
        ),
        out_specs=(P(None, ("row", "col")), P(None, ("row", "col")), P()),
        check_vma=False,
    )
```

```python
import math

import jax
import jax.numpy as jnp
from jax import lax
from jax.experimental.layout import Layout, with_layout_constraint
from jax.sharding import PartitionSpec as P

SOFT = 1.0


def sincos(angle):
    quarter = jnp.round(angle * (2.0 / math.pi))
    rest = angle - quarter * 1.5703125
    rest = rest - quarter * 4.837512969970703125e-4
    rest = rest - quarter * 7.54978995489188216e-8
    rest_sq = rest * rest
    odd = rest + rest * rest_sq * (
        -1.6666654611e-1 + rest_sq * (8.3321608736e-3 + rest_sq * -1.9515295891e-4)
    )
    even = (
        1.0
        - 0.5 * rest_sq
        + rest_sq
        * rest_sq
        * (4.166664568298827e-2 + rest_sq * (-1.388731625493765e-3 + rest_sq * 2.443315711809948e-5))
    )
    turn = quarter.astype(jnp.int32)
    swap = (turn & 1) == 1
    sine = jnp.where(swap, even, odd)
    cosine = jnp.where(swap, odd, even)
    sine = jnp.where((turn & 2) == 2, -sine, sine)
    cosine = jnp.where(((turn + 1) & 2) == 2, -cosine, cosine)
    return sine, cosine


def pair_block(target_pos, target_str, target_mu, source_pos, source_str, source_mu, wavenumbers):
    freqs = wavenumbers.shape[0]
    offset = target_pos[:, None, :] - source_pos[:, :, None]
    squared = jnp.sum(offset * offset, axis=0) + SOFT
    inverse = lax.rsqrt(squared)
    distance = squared * inverse
    phase = wavenumbers[:, None, None] * distance[None]
    sine, cosine = sincos(phase)
    tgt_real = target_str[:freqs, None, :]
    tgt_imag = target_str[freqs:, None, :]
    tmu_real = target_mu[:freqs, None, :]
    tmu_imag = target_mu[freqs:, None, :]
    src_real = source_str[:freqs, :, None]
    src_imag = source_str[freqs:, :, None]
    smu_real = source_mu[:freqs, :, None]
    smu_imag = source_mu[freqs:, :, None]
    prod_real = (
        tmu_real * src_real - tmu_imag * src_imag + smu_real * tgt_real - smu_imag * tgt_imag
    )
    prod_imag = (
        tmu_real * src_imag + tmu_imag * src_real + smu_real * tgt_imag + smu_imag * tgt_real
    )
    inner = cosine * (prod_real + phase * prod_imag) + sine * (phase * prod_real - prod_imag)
    weight = -jnp.sum(inner, axis=0) * (inverse * inverse * inverse)
    return jnp.sum(weight[None] * offset, axis=1)


def pair_sweep(
    total, target_pos, target_str, target_mu, source_pos, source_str, source_mu, wavenumbers
):
    width = source_pos.shape[1]
    step = math.gcd(width, 512)

    def visit_block(carry, block_index):
        begin = block_index * step
        spos = lax.dynamic_slice_in_dim(source_pos, begin, step, 1)
        sstr = lax.dynamic_slice_in_dim(source_str, begin, step, 1)
        smu = lax.dynamic_slice_in_dim(source_mu, begin, step, 1)
        return (
            carry + pair_block(target_pos, target_str, target_mu, spos, sstr, smu, wavenumbers),
            None,
        )

    result, _ = lax.scan(visit_block, total, jnp.arange(width // step, dtype=jnp.int32))
    return result


def complex_times(left, right, freqs):
    left_real, left_imag = (left[:freqs], left[freqs:])
    right_real, right_imag = (right[:freqs], right[freqs:])
    return jnp.concatenate(
        [
            left_real * right_real - left_imag * right_imag,
            left_real * right_imag + left_imag * right_real,
        ],
        axis=0,
    )


def row_major(value):
    return with_layout_constraint(value, Layout(tuple(range(value.ndim))))


def xor_psum(value, axis):
    count = lax.axis_size(axis)
    shift = 1
    while shift < count:
        partner = [(index, index ^ shift) for index in range(count)]
        value = row_major(value)
        value = value + lax.ppermute(value, axis, partner)
        shift *= 2
    return value


def halving_scatter(value, axis):
    count = lax.axis_size(axis)
    me = lax.axis_index(axis)
    shift = 1
    while shift < count:
        half = value.shape[1] // 2
        low, high = value[:, :half], value[:, half:]
        upper = (me // shift) % 2 == 1
        keep = jnp.where(upper, high, low)
        send = row_major(jnp.where(upper, low, high))
        partner = [(index, index ^ shift) for index in range(count)]
        value = keep + lax.ppermute(send, axis, partner)
        shift *= 2
    return value


def bit_reverse(value, bits):
    result = jnp.zeros_like(value)
    for bit in range(bits):
        result = result | (((value >> bit) & 1) << (bits - 1 - bit))
    return result


def split_three(value):
    high = lax.reduce_precision(value, exponent_bits=8, mantissa_bits=7)
    rest = value - high
    middle = lax.reduce_precision(rest, exponent_bits=8, mantissa_bits=7)
    low = rest - middle
    return jnp.concatenate([high, middle, low], axis=0).astype(jnp.bfloat16)


def join_three(value):
    rows = value.shape[0] // 3
    return (value[:rows] + value[rows : 2 * rows]) + value[2 * rows :]


def on_device(centroids, strengths, self_inv, wavenumbers, field_pos, targets, lists, connect):
    owned_count = centroids.shape[1]
    row_count = lax.axis_size("row")
    col_count = lax.axis_size("col")
    row_index = lax.axis_index("row")
    col_index = lax.axis_index("col")
    freqs = wavenumbers.shape[0]
    listed = lists.shape[1]
    panel_total = owned_count * row_count * col_count
    field_total = field_pos.shape[1] * row_count
    pos_rows = centroids.shape[0]
    str_rows = strengths.shape[0]
    owned = jnp.concatenate([centroids, strengths, self_inv], axis=0)
    src_all = lax.all_gather(owned, "row", axis=1, tiled=True)
    src_pos = src_all[:pos_rows]
    src_str = src_all[pos_rows : pos_rows + str_rows]
    src_inv = src_all[pos_rows + str_rows :]
    source_count = src_all.shape[1]
    panel_ids = lists.reshape(-1)
    owner_block = panel_ids // owned_count
    owner_row = owner_block // col_count
    mask = (owner_block % col_count == col_index).astype(jnp.float32)
    row_bits = max(row_count - 1, 0).bit_length()
    slot_ids = bit_reverse(owner_row, row_bits) * owned_count + panel_ids % owned_count
    slot_order = [
        sum(((slot >> bit) & 1) << (row_bits - 1 - bit) for bit in range(row_bits))
        for slot in range(row_count)
    ]
    table = src_all[: pos_rows + str_rows].reshape(-1, row_count, owned_count)
    table = jnp.concatenate([table[:, slot] for slot in slot_order], axis=1)
    onehot = (
        slot_ids[None, :] == lax.broadcasted_iota(jnp.int32, (source_count, slot_ids.shape[0]), 0)
    ).astype(jnp.bfloat16)
    near_all = join_three(
        jnp.dot(split_three(table), onehot, preferred_element_type=jnp.float32)
    )
    near = near_all[:pos_rows]
    observer = jnp.repeat(field_pos, listed, axis=1)
    offset = observer - near
    distance = jnp.sqrt(jnp.sum(offset * offset, axis=0) + SOFT)
    inverse = mask / distance
    phase = wavenumbers[:, None] * distance[None]
    sine, cosine = sincos(phase)
    near_str = near_all[pos_rows:]
    str_real = near_str[:freqs]
    str_imag = near_str[freqs:]
    part_real = (cosine * str_real - sine * str_imag) * inverse
    part_imag = (cosine * str_imag + sine * str_real) * inverse
    eta_part = jnp.concatenate(
        [
            part_real.reshape(freqs, -1, listed).sum(axis=2),
            part_imag.reshape(freqs, -1, listed).sum(axis=2),
        ],
        axis=0,
    )
    eta = xor_psum(eta_part, "col")
    resid = eta - targets
    rep_real = jnp.repeat(resid[:freqs], listed, axis=1)
    rep_imag = jnp.repeat(resid[freqs:], listed, axis=1)
    term_real = (cosine * rep_real + sine * rep_imag) * inverse
    term_imag = (cosine * rep_imag - sine * rep_real) * inverse
    terms = jnp.concatenate([term_real, term_imag], axis=0)
    source_part = join_three(
        lax.dot_general(
            split_three(terms),
            onehot,
            (((1,), (1,)), ((), ())),
            preferred_element_type=jnp.float32,
        )
    )
    misfit_part = jnp.sum(resid * resid)
    misfit_row = jnp.full((1, source_count), misfit_part, jnp.float32)
    packed = halving_scatter(
        jnp.concatenate([source_part, misfit_row], axis=0), "row"
    )
    objective = packed[2 * freqs, 0] / (freqs * field_total) + 1e-06
    source_own = packed[: 2 * freqs] / objective
    mu_own = complex_times(source_own, self_inv, freqs)
    mu_all = lax.all_gather(mu_own, "row", axis=1, tiled=True)
    tgt_all = lax.all_gather(
        jnp.concatenate([centroids, strengths, mu_own], axis=0), "col", axis=1, tiled=True
    )
    tgt_pos = tgt_all[:pos_rows]
    tgt_str = tgt_all[pos_rows : pos_rows + str_rows]
    tgt_mu = tgt_all[pos_rows + str_rows :]
    block_width = tgt_pos.shape[1]
    empty = jnp.zeros((3, block_width), jnp.float32)
    accum = pair_sweep(empty, tgt_pos, tgt_str, tgt_mu, src_pos, src_str, mu_all, wavenumbers)
    panel_sens = accum * (1.0 / math.sqrt(panel_total * freqs))
    vertex_local = connect - row_index * block_width
    vertex_hits = (
        vertex_local[:, None, :] == lax.broadcasted_iota(jnp.int32, (1, block_width, 1), 1)
    ).astype(jnp.bfloat16)
    vertex_part = join_three(
        jnp.einsum(
            "cp,kvp->cv",
            split_three(0.25 * panel_sens),
            vertex_hits,
            preferred_element_type=jnp.float32,
        )
    )
    lanes = 128 if block_width % 128 == 0 else block_width
    vertex_rows = vertex_part.reshape(3 * block_width // lanes, lanes)
    vertex_sum = xor_psum(vertex_rows, "col").reshape(3, block_width)
    vertex_own = lax.dynamic_slice_in_dim(vertex_sum, col_index * owned_count, owned_count, 1)
    adjoint = mu_own
    return (adjoint, vertex_own, objective)


def solution(mesh):
    return jax.shard_map(
        on_device,
        mesh=mesh,
        in_specs=(
            P(None, ("row", "col")),
            P(None, ("row", "col")),
            P(None, ("row", "col")),
            P(),
            P(None, "row"),
            P(None, "row"),
            P("row", None),
            P(None, "row"),
        ),
        out_specs=(P(None, ("row", "col")), P(None, ("row", "col")), P()),
        check_vma=False,
    )
```

```python
import math

import jax
import jax.numpy as jnp
from jax import lax
from jax.experimental.layout import Layout, with_layout_constraint
from jax.sharding import PartitionSpec as P

SOFT = 1.0


def sincos(angle):
    quarter = jnp.round(angle * (2.0 / math.pi))
    rest = angle - quarter * 1.5703125
    rest = rest - quarter * 4.838267948966e-4
    rest_sq = rest * rest
    odd = rest + rest * rest_sq * (
        -1.6666654611e-1 + rest_sq * (8.3321608736e-3 + rest_sq * -1.9515295891e-4)
    )
    even = (
        1.0
        - 0.5 * rest_sq
        + rest_sq
        * rest_sq
        * (4.166664568298827e-2 + rest_sq * (-1.388731625493765e-3 + rest_sq * 2.443315711809948e-5))
    )
    turn = quarter.astype(jnp.int32)
    swap = (turn & 1) == 1
    sine = jnp.where(swap, even, odd)
    cosine = jnp.where(swap, odd, even)
    sine = jnp.where((turn & 2) == 2, -sine, sine)
    cosine = jnp.where(((turn + 1) & 2) == 2, -cosine, cosine)
    return sine, cosine


def pair_block(target_pos, target_str, target_mu, source_pos, source_str, source_mu, wavenumbers):
    freqs = wavenumbers.shape[0]
    offset = target_pos[:, None, :] - source_pos[:, :, None]
    squared = jnp.sum(offset * offset, axis=0) + SOFT
    inverse = lax.rsqrt(squared)
    distance = squared * inverse
    phase = wavenumbers[:, None, None] * distance[None]
    sine, cosine = sincos(phase)
    tgt_real = target_str[:freqs, None, :]
    tgt_imag = target_str[freqs:, None, :]
    tmu_real = target_mu[:freqs, None, :]
    tmu_imag = target_mu[freqs:, None, :]
    src_real = source_str[:freqs, :, None]
    src_imag = source_str[freqs:, :, None]
    smu_real = source_mu[:freqs, :, None]
    smu_imag = source_mu[freqs:, :, None]
    prod_real = (
        tmu_real * src_real - tmu_imag * src_imag + smu_real * tgt_real - smu_imag * tgt_imag
    )
    prod_imag = (
        tmu_real * src_imag + tmu_imag * src_real + smu_real * tgt_imag + smu_imag * tgt_real
    )
    inner = cosine * (prod_real + phase * prod_imag) + sine * (phase * prod_real - prod_imag)
    weight = -jnp.sum(inner, axis=0) * (inverse * inverse * inverse)
    return jnp.sum(weight[None] * offset, axis=1)


def pair_sweep(
    total, target_pos, target_str, target_mu, source_pos, source_str, source_mu, wavenumbers
):
    width = source_pos.shape[1]
    step = math.gcd(width, 512)

    def visit_block(carry, block_index):
        begin = block_index * step
        spos = lax.dynamic_slice_in_dim(source_pos, begin, step, 1)
        sstr = lax.dynamic_slice_in_dim(source_str, begin, step, 1)
        smu = lax.dynamic_slice_in_dim(source_mu, begin, step, 1)
        return (
            carry + pair_block(target_pos, target_str, target_mu, spos, sstr, smu, wavenumbers),
            None,
        )

    result, _ = lax.scan(visit_block, total, jnp.arange(width // step, dtype=jnp.int32))
    return result


def complex_times(left, right, freqs):
    left_real, left_imag = (left[:freqs], left[freqs:])
    right_real, right_imag = (right[:freqs], right[freqs:])
    return jnp.concatenate(
        [
            left_real * right_real - left_imag * right_imag,
            left_real * right_imag + left_imag * right_real,
        ],
        axis=0,
    )


def row_major(value):
    return with_layout_constraint(value, Layout(tuple(range(value.ndim))))


def xor_psum(value, axis):
    count = lax.axis_size(axis)
    shift = 1
    while shift < count:
        partner = [(index, index ^ shift) for index in range(count)]
        value = row_major(value)
        value = value + lax.ppermute(value, axis, partner)
        shift *= 2
    return value


def halving_scatter(value, axis):
    count = lax.axis_size(axis)
    me = lax.axis_index(axis)
    shift = 1
    while shift < count:
        half = value.shape[1] // 2
        low, high = value[:, :half], value[:, half:]
        upper = (me // shift) % 2 == 1
        keep = jnp.where(upper, high, low)
        send = row_major(jnp.where(upper, low, high))
        partner = [(index, index ^ shift) for index in range(count)]
        value = keep + lax.ppermute(send, axis, partner)
        shift *= 2
    return value


def bit_reverse(value, bits):
    result = jnp.zeros_like(value)
    for bit in range(bits):
        result = result | (((value >> bit) & 1) << (bits - 1 - bit))
    return result


def near_far_psum(value, axis, near):
    count = lax.axis_size(axis)
    me = lax.axis_index(axis)
    shift = 1
    while shift < near:
        half = value.shape[1] // 2
        low, high = value[:, :half], value[:, half:]
        upper = (me // shift) % 2 == 1
        keep = jnp.where(upper, high, low)
        send = row_major(jnp.where(upper, low, high))
        partner = [(index, index ^ shift) for index in range(count)]
        value = keep + lax.ppermute(send, axis, partner)
        shift *= 2
    while shift < count:
        value = row_major(value)
        partner = [(index, index ^ shift) for index in range(count)]
        value = value + lax.ppermute(value, axis, partner)
        shift *= 2
    shift = near // 2
    while shift >= 1:
        upper = (me // shift) % 2 == 1
        value = row_major(value)
        partner = [(index, index ^ shift) for index in range(count)]
        other = lax.ppermute(value, axis, partner)
        value = jnp.where(
            upper,
            jnp.concatenate([other, value], axis=1),
            jnp.concatenate([value, other], axis=1),
        )
        shift //= 2
    return value


def split_three(value):
    high = lax.reduce_precision(value, exponent_bits=8, mantissa_bits=7)
    rest = value - high
    middle = lax.reduce_precision(rest, exponent_bits=8, mantissa_bits=7)
    low = rest - middle
    return jnp.concatenate([high, middle, low], axis=0).astype(jnp.bfloat16)


def join_three(value):
    rows = value.shape[0] // 3
    return (value[:rows] + value[rows : 2 * rows]) + value[2 * rows :]


def on_device(centroids, strengths, self_inv, wavenumbers, field_pos, targets, lists, connect):
    owned_count = centroids.shape[1]
    row_count = lax.axis_size("row")
    col_count = lax.axis_size("col")
    row_index = lax.axis_index("row")
    col_index = lax.axis_index("col")
    freqs = wavenumbers.shape[0]
    listed = lists.shape[1]
    panel_total = owned_count * row_count * col_count
    field_total = field_pos.shape[1] * row_count
    pos_rows = centroids.shape[0]
    str_rows = strengths.shape[0]
    owned = jnp.concatenate([centroids, strengths, self_inv], axis=0)
    src_all = lax.all_gather(owned, "row", axis=1, tiled=True)
    source_count = src_all.shape[1]
    panel_ids = lists.reshape(-1)
    owner_block = panel_ids // owned_count
    owner_row = owner_block // col_count
    mask = (owner_block % col_count == col_index).astype(jnp.float32)
    row_bits = max(row_count - 1, 0).bit_length()
    slot_ids = bit_reverse(owner_row, row_bits) * owned_count + panel_ids % owned_count
    slot_order = [
        sum(((slot >> bit) & 1) << (row_bits - 1 - bit) for bit in range(row_bits))
        for slot in range(row_count)
    ]
    table = src_all.reshape(-1, row_count, owned_count)
    table = jnp.concatenate([table[:, slot] for slot in slot_order], axis=1)
    src_pos = table[:pos_rows]
    src_str = table[pos_rows : pos_rows + str_rows]
    src_inv = table[pos_rows + str_rows :]
    onehot = (
        slot_ids[None, :] == lax.broadcasted_iota(jnp.int32, (source_count, slot_ids.shape[0]), 0)
    ).astype(jnp.bfloat16)
    near_all = join_three(
        jnp.dot(split_three(table[: pos_rows + str_rows]), onehot, preferred_element_type=jnp.float32)
    )
    near = near_all[:pos_rows]
    observer = jnp.repeat(field_pos, listed, axis=1)
    offset = observer - near
    distance = jnp.sqrt(jnp.sum(offset * offset, axis=0) + SOFT)
    inverse = mask / distance
    phase = wavenumbers[:, None] * distance[None]
    sine, cosine = sincos(phase)
    near_str = near_all[pos_rows:]
    str_real = near_str[:freqs]
    str_imag = near_str[freqs:]
    part_real = (cosine * str_real - sine * str_imag) * inverse
    part_imag = (cosine * str_imag + sine * str_real) * inverse
    eta_part = jnp.concatenate(
        [
            part_real.reshape(freqs, -1, listed).sum(axis=2),
            part_imag.reshape(freqs, -1, listed).sum(axis=2),
        ],
        axis=0,
    )
    eta = xor_psum(eta_part, "col")
    resid = eta - targets
    rep_real = jnp.repeat(resid[:freqs], listed, axis=1)
    rep_imag = jnp.repeat(resid[freqs:], listed, axis=1)
    term_real = (cosine * rep_real + sine * rep_imag) * inverse
    term_imag = (cosine * rep_imag - sine * rep_real) * inverse
    terms = jnp.concatenate([term_real, term_imag], axis=0)
    source_part = join_three(
        lax.dot_general(
            split_three(terms),
            onehot,
            (((1,), (1,)), ((), ())),
            preferred_element_type=jnp.float32,
        )
    )
    misfit_part = jnp.sum(resid * resid)
    misfit_row = jnp.full((1, source_count), misfit_part, jnp.float32)
    packed = near_far_psum(
        jnp.concatenate([source_part, misfit_row], axis=0), "row", min(8, row_count)
    )
    objective = packed[2 * freqs, 0] / (freqs * field_total) + 1e-06
    mu_all = complex_times(packed[: 2 * freqs] / objective, src_inv, freqs)
    own_slot = bit_reverse(row_index, row_bits) * owned_count
    mu_own = lax.dynamic_slice_in_dim(mu_all, own_slot, owned_count, 1)
    tgt_all = lax.all_gather(
        jnp.concatenate([centroids, strengths, mu_own], axis=0), "col", axis=1, tiled=True
    )
    tgt_pos = tgt_all[:pos_rows]
    tgt_str = tgt_all[pos_rows : pos_rows + str_rows]
    tgt_mu = tgt_all[pos_rows + str_rows :]
    block_width = tgt_pos.shape[1]
    empty = jnp.zeros((3, block_width), jnp.float32)
    accum = pair_sweep(empty, tgt_pos, tgt_str, tgt_mu, src_pos, src_str, mu_all, wavenumbers)
    panel_sens = accum * (1.0 / math.sqrt(panel_total * freqs))
    vertex_local = connect - row_index * block_width
    vertex_hits = (
        vertex_local[:, None, :] == lax.broadcasted_iota(jnp.int32, (1, block_width, 1), 1)
    ).astype(jnp.bfloat16)
    vertex_part = join_three(
        jnp.einsum(
            "cp,kvp->cv",
            split_three(0.25 * panel_sens),
            vertex_hits,
            preferred_element_type=jnp.float32,
        )
    )
    lanes = 128 if block_width % 128 == 0 else block_width
    vertex_rows = vertex_part.reshape(3 * block_width // lanes, lanes)
    vertex_sum = xor_psum(vertex_rows, "col").reshape(3, block_width)
    vertex_own = lax.dynamic_slice_in_dim(vertex_sum, col_index * owned_count, owned_count, 1)
    adjoint = mu_own
    return (adjoint, vertex_own, objective)


def solution(mesh):
    return jax.shard_map(
        on_device,
        mesh=mesh,
        in_specs=(
            P(None, ("row", "col")),
            P(None, ("row", "col")),
            P(None, ("row", "col")),
            P(),
            P(None, "row"),
            P(None, "row"),
            P("row", None),
            P(None, "row"),
        ),
        out_specs=(P(None, ("row", "col")), P(None, ("row", "col")), P()),
        check_vma=False,
    )
```

```python
import math

import jax
import jax.numpy as jnp
from jax import lax
from jax.experimental.layout import Layout, with_layout_constraint
from jax.sharding import PartitionSpec as P

SOFT = 1.0


def sincos_parts(angle):
    quarter = jnp.round(angle * (2.0 / math.pi))
    rest = angle - quarter * 1.5703125
    rest = rest - quarter * 4.838267948966e-4
    rest_sq = rest * rest
    odd = rest + rest * rest_sq * (
        -1.6666654611e-1 + rest_sq * (8.3321608736e-3 + rest_sq * -1.9515295891e-4)
    )
    even = (
        1.0
        - 0.5 * rest_sq
        + rest_sq
        * rest_sq
        * (4.166664568298827e-2 + rest_sq * (-1.388731625493765e-3 + rest_sq * 2.443315711809948e-5))
    )
    return odd, even, quarter.astype(jnp.int32)


def sincos(angle):
    odd, even, turn = sincos_parts(angle)
    swap = (turn & 1) == 1
    sine = jnp.where(swap, even, odd)
    cosine = jnp.where(swap, odd, even)
    sine = jnp.where((turn & 2) == 2, -sine, sine)
    cosine = jnp.where(((turn + 1) & 2) == 2, -cosine, cosine)
    return sine, cosine


def pair_block(target_pos, target_str, target_mu, source_pos, source_str, source_mu, wavenumbers):
    freqs = wavenumbers.shape[0]
    offset = target_pos[:, None, :] - source_pos[:, :, None]
    squared = jnp.sum(offset * offset, axis=0) + SOFT
    inverse = lax.rsqrt(squared)
    distance = squared * inverse
    phase = wavenumbers[:, None, None] * distance[None]
    odd, even, turn = sincos_parts(phase)
    tgt_real = target_str[:freqs, None, :]
    tgt_imag = target_str[freqs:, None, :]
    tmu_real = target_mu[:freqs, None, :]
    tmu_imag = target_mu[freqs:, None, :]
    src_real = source_str[:freqs, :, None]
    src_imag = source_str[freqs:, :, None]
    smu_real = source_mu[:freqs, :, None]
    smu_imag = source_mu[freqs:, :, None]
    prod_real = (
        tmu_real * src_real - tmu_imag * src_imag + smu_real * tgt_real - smu_imag * tgt_imag
    )
    prod_imag = (
        tmu_real * src_imag + tmu_imag * src_real + smu_real * tgt_imag + smu_imag * tgt_real
    )
    first = prod_real + phase * prod_imag
    second = phase * prod_real - prod_imag
    swap = (turn & 1) == 1
    inner = even * jnp.where(swap, second, first) + odd * jnp.where(swap, -first, second)
    inner = jnp.where((turn & 2) == 2, inner, -inner)
    weight = jnp.sum(inner, axis=0) * (inverse * inverse * inverse)
    return jnp.sum(weight[None] * offset, axis=1)


def pair_sweep(
    total, target_pos, target_str, target_mu, source_pos, source_str, source_mu, wavenumbers
):
    width = source_pos.shape[1]
    step = math.gcd(width, 512)

    def visit_block(carry, block_index):
        begin = block_index * step
        spos = lax.dynamic_slice_in_dim(source_pos, begin, step, 1)
        sstr = lax.dynamic_slice_in_dim(source_str, begin, step, 1)
        smu = lax.dynamic_slice_in_dim(source_mu, begin, step, 1)
        return (
            carry + pair_block(target_pos, target_str, target_mu, spos, sstr, smu, wavenumbers),
            None,
        )

    result, _ = lax.scan(visit_block, total, jnp.arange(width // step, dtype=jnp.int32))
    return result


def complex_times(left, right, freqs):
    left_real, left_imag = (left[:freqs], left[freqs:])
    right_real, right_imag = (right[:freqs], right[freqs:])
    return jnp.concatenate(
        [
            left_real * right_real - left_imag * right_imag,
            left_real * right_imag + left_imag * right_real,
        ],
        axis=0,
    )


def row_major(value):
    return with_layout_constraint(value, Layout(tuple(range(value.ndim))))


def xor_psum(value, axis):
    count = lax.axis_size(axis)
    shift = 1
    while shift < count:
        partner = [(index, index ^ shift) for index in range(count)]
        value = row_major(value)
        value = value + lax.ppermute(value, axis, partner)
        shift *= 2
    return value


def halving_scatter(value, axis):
    count = lax.axis_size(axis)
    me = lax.axis_index(axis)
    shift = 1
    while shift < count:
        half = value.shape[1] // 2
        low, high = value[:, :half], value[:, half:]
        upper = (me // shift) % 2 == 1
        keep = jnp.where(upper, high, low)
        send = row_major(jnp.where(upper, low, high))
        partner = [(index, index ^ shift) for index in range(count)]
        value = keep + lax.ppermute(send, axis, partner)
        shift *= 2
    return value


def bit_reverse(value, bits):
    result = jnp.zeros_like(value)
    for bit in range(bits):
        result = result | (((value >> bit) & 1) << (bits - 1 - bit))
    return result


def near_far_psum(value, axis, near):
    count = lax.axis_size(axis)
    me = lax.axis_index(axis)
    shift = 1
    while shift < near:
        half = value.shape[1] // 2
        low, high = value[:, :half], value[:, half:]
        upper = (me // shift) % 2 == 1
        keep = jnp.where(upper, high, low)
        send = row_major(jnp.where(upper, low, high))
        partner = [(index, index ^ shift) for index in range(count)]
        value = keep + lax.ppermute(send, axis, partner)
        shift *= 2
    while shift < count:
        value = row_major(value)
        partner = [(index, index ^ shift) for index in range(count)]
        value = value + lax.ppermute(value, axis, partner)
        shift *= 2
    shift = near // 2
    while shift >= 1:
        upper = (me // shift) % 2 == 1
        value = row_major(value)
        partner = [(index, index ^ shift) for index in range(count)]
        other = lax.ppermute(value, axis, partner)
        value = jnp.where(
            upper,
            jnp.concatenate([other, value], axis=1),
            jnp.concatenate([value, other], axis=1),
        )
        shift //= 2
    return value


def split_three(value):
    high = lax.reduce_precision(value, exponent_bits=8, mantissa_bits=7)
    rest = value - high
    middle = lax.reduce_precision(rest, exponent_bits=8, mantissa_bits=7)
    low = rest - middle
    return jnp.concatenate([high, middle, low], axis=0).astype(jnp.bfloat16)


def join_three(value):
    rows = value.shape[0] // 3
    return (value[:rows] + value[rows : 2 * rows]) + value[2 * rows :]


def on_device(centroids, strengths, self_inv, wavenumbers, field_pos, targets, lists, connect):
    owned_count = centroids.shape[1]
    row_count = lax.axis_size("row")
    col_count = lax.axis_size("col")
    row_index = lax.axis_index("row")
    col_index = lax.axis_index("col")
    freqs = wavenumbers.shape[0]
    listed = lists.shape[1]
    panel_total = owned_count * row_count * col_count
    field_total = field_pos.shape[1] * row_count
    pos_rows = centroids.shape[0]
    str_rows = strengths.shape[0]
    owned = jnp.concatenate([centroids, strengths, self_inv], axis=0)
    src_all = lax.all_gather(owned, "row", axis=1, tiled=True)
    source_count = src_all.shape[1]
    panel_ids = lists.reshape(-1)
    owner_block = panel_ids // owned_count
    owner_row = owner_block // col_count
    mask = (owner_block % col_count == col_index).astype(jnp.float32)
    row_bits = max(row_count - 1, 0).bit_length()
    slot_ids = bit_reverse(owner_row, row_bits) * owned_count + panel_ids % owned_count
    slot_order = [
        sum(((slot >> bit) & 1) << (row_bits - 1 - bit) for bit in range(row_bits))
        for slot in range(row_count)
    ]
    table = src_all.reshape(-1, row_count, owned_count)
    table = jnp.concatenate([table[:, slot] for slot in slot_order], axis=1)
    src_pos = table[:pos_rows]
    src_str = table[pos_rows : pos_rows + str_rows]
    src_inv = table[pos_rows + str_rows :]
    onehot = (
        slot_ids[None, :] == lax.broadcasted_iota(jnp.int32, (source_count, slot_ids.shape[0]), 0)
    ).astype(jnp.bfloat16)
    near_all = join_three(
        jnp.dot(split_three(table[: pos_rows + str_rows]), onehot, preferred_element_type=jnp.float32)
    )
    near = near_all[:pos_rows]
    observer = jnp.repeat(field_pos, listed, axis=1)
    offset = observer - near
    distance = jnp.sqrt(jnp.sum(offset * offset, axis=0) + SOFT)
    inverse = mask / distance
    phase = wavenumbers[:, None] * distance[None]
    sine, cosine = sincos(phase)
    near_str = near_all[pos_rows:]
    str_real = near_str[:freqs]
    str_imag = near_str[freqs:]
    part_real = (cosine * str_real - sine * str_imag) * inverse
    part_imag = (cosine * str_imag + sine * str_real) * inverse
    eta_part = jnp.concatenate(
        [
            part_real.reshape(freqs, -1, listed).sum(axis=2),
            part_imag.reshape(freqs, -1, listed).sum(axis=2),
        ],
        axis=0,
    )
    eta = xor_psum(eta_part, "col")
    resid = eta - targets
    rep_real = jnp.repeat(resid[:freqs], listed, axis=1)
    rep_imag = jnp.repeat(resid[freqs:], listed, axis=1)
    term_real = (cosine * rep_real + sine * rep_imag) * inverse
    term_imag = (cosine * rep_imag - sine * rep_real) * inverse
    terms = jnp.concatenate([term_real, term_imag], axis=0)
    source_part = join_three(
        lax.dot_general(
            split_three(terms),
            onehot,
            (((1,), (1,)), ((), ())),
            preferred_element_type=jnp.float32,
        )
    )
    misfit_part = jnp.sum(resid * resid)
    misfit_row = jnp.full((1, source_count), misfit_part, jnp.float32)
    packed = near_far_psum(
        jnp.concatenate([source_part, misfit_row], axis=0), "row", min(8, row_count)
    )
    objective = packed[2 * freqs, 0] / (freqs * field_total) + 1e-06
    mu_all = complex_times(packed[: 2 * freqs] / objective, src_inv, freqs)
    own_slot = bit_reverse(row_index, row_bits) * owned_count
    mu_own = lax.dynamic_slice_in_dim(mu_all, own_slot, owned_count, 1)
    tgt_all = lax.all_gather(
        jnp.concatenate([centroids, strengths, mu_own], axis=0), "col", axis=1, tiled=True
    )
    tgt_pos = tgt_all[:pos_rows]
    tgt_str = tgt_all[pos_rows : pos_rows + str_rows]
    tgt_mu = tgt_all[pos_rows + str_rows :]
    block_width = tgt_pos.shape[1]
    empty = jnp.zeros((3, block_width), jnp.float32)
    accum = pair_sweep(empty, tgt_pos, tgt_str, tgt_mu, src_pos, src_str, mu_all, wavenumbers)
    panel_sens = accum * (1.0 / math.sqrt(panel_total * freqs))
    vertex_local = connect - row_index * block_width
    vertex_hits = (
        vertex_local[:, None, :] == lax.broadcasted_iota(jnp.int32, (1, block_width, 1), 1)
    ).astype(jnp.bfloat16)
    vertex_part = join_three(
        jnp.einsum(
            "cp,kvp->cv",
            split_three(0.25 * panel_sens),
            vertex_hits,
            preferred_element_type=jnp.float32,
        )
    )
    lanes = 128 if block_width % 128 == 0 else block_width
    vertex_rows = vertex_part.reshape(3 * block_width // lanes, lanes)
    vertex_sum = xor_psum(vertex_rows, "col").reshape(3, block_width)
    vertex_own = lax.dynamic_slice_in_dim(vertex_sum, col_index * owned_count, owned_count, 1)
    adjoint = mu_own
    return (adjoint, vertex_own, objective)


def solution(mesh):
    return jax.shard_map(
        on_device,
        mesh=mesh,
        in_specs=(
            P(None, ("row", "col")),
            P(None, ("row", "col")),
            P(None, ("row", "col")),
            P(),
            P(None, "row"),
            P(None, "row"),
            P("row", None),
            P(None, "row"),
        ),
        out_specs=(P(None, ("row", "col")), P(None, ("row", "col")), P()),
        check_vma=False,
    )
```

```python
import math

import jax
import jax.numpy as jnp
from jax import lax
from jax.experimental.layout import Layout, with_layout_constraint
from jax.sharding import PartitionSpec as P

SOFT = 1.0


def sincos_parts(angle):
    quarter = jnp.round(angle * (2.0 / math.pi))
    rest = angle - quarter * 1.5703125
    rest = rest - quarter * 4.838267948966e-4
    rest_sq = rest * rest
    odd = rest + rest * rest_sq * (
        -1.6666654611e-1 + rest_sq * (8.3321608736e-3 + rest_sq * -1.9515295891e-4)
    )
    even = (
        1.0
        - 0.5 * rest_sq
        + rest_sq
        * rest_sq
        * (4.166664568298827e-2 + rest_sq * (-1.388731625493765e-3 + rest_sq * 2.443315711809948e-5))
    )
    return odd, even, quarter.astype(jnp.int32)


def sincos(angle):
    odd, even, turn = sincos_parts(angle)
    swap = (turn & 1) == 1
    sine = jnp.where(swap, even, odd)
    cosine = jnp.where(swap, odd, even)
    sine = jnp.where((turn & 2) == 2, -sine, sine)
    cosine = jnp.where(((turn + 1) & 2) == 2, -cosine, cosine)
    return sine, cosine


def pair_block(target_pos, target_str, target_mu, source_pos, source_str, source_mu, wavenumbers):
    freqs = wavenumbers.shape[0]
    offset = target_pos[:, None, :] - source_pos[:, :, None]
    squared = jnp.sum(offset * offset, axis=0) + SOFT
    inverse = lax.rsqrt(squared)
    distance = squared * inverse
    phase = wavenumbers[:, None, None] * distance[None]
    odd, even, turn = sincos_parts(phase)
    tgt_real = target_str[:freqs, None, :]
    tgt_imag = target_str[freqs:, None, :]
    tmu_real = target_mu[:freqs, None, :]
    tmu_imag = target_mu[freqs:, None, :]
    src_real = source_str[:freqs, :, None]
    src_imag = source_str[freqs:, :, None]
    smu_real = source_mu[:freqs, :, None]
    smu_imag = source_mu[freqs:, :, None]
    prod_real = (
        tmu_real * src_real - tmu_imag * src_imag + smu_real * tgt_real - smu_imag * tgt_imag
    )
    prod_imag = (
        tmu_real * src_imag + tmu_imag * src_real + smu_real * tgt_imag + smu_imag * tgt_real
    )
    first = prod_real + phase * prod_imag
    second = phase * prod_real - prod_imag
    swap = (turn & 1) == 1
    inner = even * jnp.where(swap, second, first) + odd * jnp.where(swap, -first, second)
    inner = jnp.where((turn & 2) == 2, inner, -inner)
    weight = jnp.sum(inner, axis=0) * (inverse * inverse * inverse)
    return jnp.sum(weight[None] * offset, axis=1)


def pair_sweep(
    total, target_pos, target_str, target_mu, source_pos, source_str, source_mu, wavenumbers
):
    width = source_pos.shape[1]
    step = math.gcd(width, 512)

    def visit_block(carry, block_index):
        begin = block_index * step
        spos = lax.dynamic_slice_in_dim(source_pos, begin, step, 1)
        sstr = lax.dynamic_slice_in_dim(source_str, begin, step, 1)
        smu = lax.dynamic_slice_in_dim(source_mu, begin, step, 1)
        return (
            carry + pair_block(target_pos, target_str, target_mu, spos, sstr, smu, wavenumbers),
            None,
        )

    result, _ = lax.scan(visit_block, total, jnp.arange(width // step, dtype=jnp.int32))
    return result


def complex_times(left, right, freqs):
    left_real, left_imag = (left[:freqs], left[freqs:])
    right_real, right_imag = (right[:freqs], right[freqs:])
    return jnp.concatenate(
        [
            left_real * right_real - left_imag * right_imag,
            left_real * right_imag + left_imag * right_real,
        ],
        axis=0,
    )


def row_major(value):
    return with_layout_constraint(value, Layout(tuple(range(value.ndim))))


def xor_psum(value, axis):
    count = lax.axis_size(axis)
    shift = 1
    while shift < count:
        partner = [(index, index ^ shift) for index in range(count)]
        value = row_major(value)
        value = value + lax.ppermute(value, axis, partner)
        shift *= 2
    return value


def halving_scatter(value, axis):
    count = lax.axis_size(axis)
    me = lax.axis_index(axis)
    shift = 1
    while shift < count:
        half = value.shape[1] // 2
        low, high = value[:, :half], value[:, half:]
        upper = (me // shift) % 2 == 1
        keep = jnp.where(upper, high, low)
        send = row_major(jnp.where(upper, low, high))
        partner = [(index, index ^ shift) for index in range(count)]
        value = keep + lax.ppermute(send, axis, partner)
        shift *= 2
    return value


def bit_reverse(value, bits):
    result = jnp.zeros_like(value)
    for bit in range(bits):
        result = result | (((value >> bit) & 1) << (bits - 1 - bit))
    return result


def near_far_reduce(value, axis, near):
    count = lax.axis_size(axis)
    me = lax.axis_index(axis)
    shift = 1
    while shift < near:
        half = value.shape[1] // 2
        low, high = value[:, :half], value[:, half:]
        upper = (me // shift) % 2 == 1
        keep = jnp.where(upper, high, low)
        send = row_major(jnp.where(upper, low, high))
        partner = [(index, index ^ shift) for index in range(count)]
        value = keep + lax.ppermute(send, axis, partner)
        shift *= 2
    while shift < count:
        value = row_major(value)
        partner = [(index, index ^ shift) for index in range(count)]
        value = value + lax.ppermute(value, axis, partner)
        shift *= 2
    return value


def doubling_gather(value, axis, shifts):
    count = lax.axis_size(axis)
    me = lax.axis_index(axis)
    for shift in shifts:
        upper = (me // shift) % 2 == 1
        value = row_major(value)
        partner = [(index, index ^ shift) for index in range(count)]
        other = lax.ppermute(value, axis, partner)
        value = jnp.where(
            upper,
            jnp.concatenate([other, value], axis=1),
            jnp.concatenate([value, other], axis=1),
        )
    return value


def near_shifts(near):
    shifts = []
    shift = near // 2
    while shift >= 1:
        shifts.append(shift)
        shift //= 2
    return shifts


def split_three(value):
    high = lax.reduce_precision(value, exponent_bits=8, mantissa_bits=7)
    rest = value - high
    middle = lax.reduce_precision(rest, exponent_bits=8, mantissa_bits=7)
    low = rest - middle
    return jnp.concatenate([high, middle, low], axis=0).astype(jnp.bfloat16)


def join_three(value):
    rows = value.shape[0] // 3
    return (value[:rows] + value[rows : 2 * rows]) + value[2 * rows :]


def on_device(centroids, strengths, self_inv, wavenumbers, field_pos, targets, lists, connect):
    owned_count = centroids.shape[1]
    row_count = lax.axis_size("row")
    col_count = lax.axis_size("col")
    row_index = lax.axis_index("row")
    col_index = lax.axis_index("col")
    freqs = wavenumbers.shape[0]
    listed = lists.shape[1]
    panel_total = owned_count * row_count * col_count
    field_total = field_pos.shape[1] * row_count
    pos_rows = centroids.shape[0]
    str_rows = strengths.shape[0]
    owned = jnp.concatenate([centroids, strengths, self_inv], axis=0)
    src_all = lax.all_gather(owned, "row", axis=1, tiled=True)
    source_count = src_all.shape[1]
    panel_ids = lists.reshape(-1)
    owner_block = panel_ids // owned_count
    owner_row = owner_block // col_count
    mask = (owner_block % col_count == col_index).astype(jnp.float32)
    row_bits = max(row_count - 1, 0).bit_length()
    slot_ids = bit_reverse(owner_row, row_bits) * owned_count + panel_ids % owned_count
    slot_order = [
        sum(((slot >> bit) & 1) << (row_bits - 1 - bit) for bit in range(row_bits))
        for slot in range(row_count)
    ]
    table = src_all.reshape(-1, row_count, owned_count)
    table = jnp.concatenate([table[:, slot] for slot in slot_order], axis=1)
    src_pos = table[:pos_rows]
    src_str = table[pos_rows : pos_rows + str_rows]
    src_inv = table[pos_rows + str_rows :]
    onehot = (
        slot_ids[None, :] == lax.broadcasted_iota(jnp.int32, (source_count, slot_ids.shape[0]), 0)
    ).astype(jnp.bfloat16)
    near_all = join_three(
        jnp.dot(split_three(table[: pos_rows + str_rows]), onehot, preferred_element_type=jnp.float32)
    )
    near = near_all[:pos_rows]
    observer = jnp.repeat(field_pos, listed, axis=1)
    offset = observer - near
    distance = jnp.sqrt(jnp.sum(offset * offset, axis=0) + SOFT)
    inverse = mask / distance
    phase = wavenumbers[:, None] * distance[None]
    sine, cosine = sincos(phase)
    near_str = near_all[pos_rows:]
    str_real = near_str[:freqs]
    str_imag = near_str[freqs:]
    part_real = (cosine * str_real - sine * str_imag) * inverse
    part_imag = (cosine * str_imag + sine * str_real) * inverse
    eta_part = jnp.concatenate(
        [
            part_real.reshape(freqs, -1, listed).sum(axis=2),
            part_imag.reshape(freqs, -1, listed).sum(axis=2),
        ],
        axis=0,
    )
    eta = xor_psum(eta_part, "col")
    resid = eta - targets
    rep_real = jnp.repeat(resid[:freqs], listed, axis=1)
    rep_imag = jnp.repeat(resid[freqs:], listed, axis=1)
    term_real = (cosine * rep_real + sine * rep_imag) * inverse
    term_imag = (cosine * rep_imag - sine * rep_real) * inverse
    terms = jnp.concatenate([term_real, term_imag], axis=0)
    source_part = join_three(
        lax.dot_general(
            split_three(terms),
            onehot,
            (((1,), (1,)), ((), ())),
            preferred_element_type=jnp.float32,
        )
    )
    misfit_part = jnp.sum(resid * resid)
    misfit_row = jnp.full((1, source_count), misfit_part, jnp.float32)
    near = min(8, row_count)
    chunk = near_far_reduce(jnp.concatenate([source_part, misfit_row], axis=0), "row", near)
    objective = chunk[2 * freqs, 0] / (freqs * field_total) + 1e-06
    own_slot = bit_reverse(row_index, row_bits) * owned_count
    own_offset = own_slot % chunk.shape[1]
    mu_own = complex_times(
        lax.dynamic_slice_in_dim(chunk[: 2 * freqs], own_offset, owned_count, 1) / objective,
        self_inv,
        freqs,
    )
    packed = doubling_gather(chunk, "row", near_shifts(near))
    mu_all = complex_times(packed[: 2 * freqs] / objective, src_inv, freqs)
    col_shifts = [1 << bit for bit in range(max(col_count - 1, 0).bit_length())]
    tgt_all = doubling_gather(
        jnp.concatenate([centroids, strengths, mu_own], axis=0), "col", col_shifts
    )
    tgt_pos = tgt_all[:pos_rows]
    tgt_str = tgt_all[pos_rows : pos_rows + str_rows]
    tgt_mu = tgt_all[pos_rows + str_rows :]
    block_width = tgt_pos.shape[1]
    empty = jnp.zeros((3, block_width), jnp.float32)
    accum = pair_sweep(empty, tgt_pos, tgt_str, tgt_mu, src_pos, src_str, mu_all, wavenumbers)
    panel_sens = accum * (1.0 / math.sqrt(panel_total * freqs))
    vertex_local = connect - row_index * block_width
    vertex_hits = (
        vertex_local[:, None, :] == lax.broadcasted_iota(jnp.int32, (1, block_width, 1), 1)
    ).astype(jnp.bfloat16)
    vertex_part = join_three(
        jnp.einsum(
            "cp,kvp->cv",
            split_three(0.25 * panel_sens),
            vertex_hits,
            preferred_element_type=jnp.float32,
        )
    )
    lanes = 128 if block_width % 128 == 0 else block_width
    vertex_rows = vertex_part.reshape(3 * block_width // lanes, lanes)
    vertex_sum = xor_psum(vertex_rows, "col").reshape(3, block_width)
    vertex_own = lax.dynamic_slice_in_dim(vertex_sum, col_index * owned_count, owned_count, 1)
    adjoint = mu_own
    return (adjoint, vertex_own, objective)


def solution(mesh):
    return jax.shard_map(
        on_device,
        mesh=mesh,
        in_specs=(
            P(None, ("row", "col")),
            P(None, ("row", "col")),
            P(None, ("row", "col")),
            P(),
            P(None, "row"),
            P(None, "row"),
            P("row", None),
            P(None, "row"),
        ),
        out_specs=(P(None, ("row", "col")), P(None, ("row", "col")), P()),
        check_vma=False,
    )
```

```python
import math

import jax
import jax.numpy as jnp
from jax import lax
from jax.experimental.layout import Layout, with_layout_constraint
from jax.sharding import PartitionSpec as P

SOFT = 1.0


def sincos_parts(angle):
    quarter = jnp.round(angle * (2.0 / math.pi))
    rest = angle - quarter * 1.5703125
    rest = rest - quarter * 4.838267948966e-4
    rest_sq = rest * rest
    odd = rest + rest * rest_sq * (
        -1.6666654611e-1 + rest_sq * (8.3321608736e-3 + rest_sq * -1.9515295891e-4)
    )
    even = (
        1.0
        - 0.5 * rest_sq
        + rest_sq
        * rest_sq
        * (4.166664568298827e-2 + rest_sq * (-1.388731625493765e-3 + rest_sq * 2.443315711809948e-5))
    )
    return odd, even, quarter.astype(jnp.int32)


def sincos(angle):
    odd, even, turn = sincos_parts(angle)
    swap = (turn & 1) == 1
    sine = jnp.where(swap, even, odd)
    cosine = jnp.where(swap, odd, even)
    sine = jnp.where((turn & 2) == 2, -sine, sine)
    cosine = jnp.where(((turn + 1) & 2) == 2, -cosine, cosine)
    return sine, cosine


def pair_block(target_pos, target_str, target_mu, source_pos, source_str, source_mu, wavenumbers):
    freqs = wavenumbers.shape[0]
    offset = target_pos[:, None, :] - source_pos[:, :, None]
    squared = jnp.sum(offset * offset, axis=0) + SOFT
    inverse = lax.rsqrt(squared)
    distance = squared * inverse
    phase = wavenumbers[:, None, None] * distance[None]
    odd, even, turn = sincos_parts(phase)
    tgt_real = target_str[:freqs, None, :]
    tgt_imag = target_str[freqs:, None, :]
    tmu_real = target_mu[:freqs, None, :]
    tmu_imag = target_mu[freqs:, None, :]
    src_real = source_str[:freqs, :, None]
    src_imag = source_str[freqs:, :, None]
    smu_real = source_mu[:freqs, :, None]
    smu_imag = source_mu[freqs:, :, None]
    prod_real = (
        tmu_real * src_real - tmu_imag * src_imag + smu_real * tgt_real - smu_imag * tgt_imag
    )
    prod_imag = (
        tmu_real * src_imag + tmu_imag * src_real + smu_real * tgt_imag + smu_imag * tgt_real
    )
    first = prod_real + phase * prod_imag
    second = phase * prod_real - prod_imag
    swap = (turn & 1) == 1
    inner = even * jnp.where(swap, second, first) + odd * jnp.where(swap, -first, second)
    inner = jnp.where((turn & 2) == 2, inner, -inner)
    weight = jnp.sum(inner, axis=0) * (inverse * inverse * inverse)
    return jnp.sum(weight[None] * offset, axis=1)


def pair_sweep(
    total, target_pos, target_str, target_mu, source_pos, source_str, source_mu, wavenumbers
):
    width = source_pos.shape[1]
    step = math.gcd(width, 512)

    def visit_block(carry, block_index):
        begin = block_index * step
        spos = lax.dynamic_slice_in_dim(source_pos, begin, step, 1)
        sstr = lax.dynamic_slice_in_dim(source_str, begin, step, 1)
        smu = lax.dynamic_slice_in_dim(source_mu, begin, step, 1)
        return (
            carry + pair_block(target_pos, target_str, target_mu, spos, sstr, smu, wavenumbers),
            None,
        )

    result, _ = lax.scan(visit_block, total, jnp.arange(width // step, dtype=jnp.int32))
    return result


def complex_times(left, right, freqs):
    left_real, left_imag = (left[:freqs], left[freqs:])
    right_real, right_imag = (right[:freqs], right[freqs:])
    return jnp.concatenate(
        [
            left_real * right_real - left_imag * right_imag,
            left_real * right_imag + left_imag * right_real,
        ],
        axis=0,
    )


def row_major(value):
    return with_layout_constraint(value, Layout(tuple(range(value.ndim))))


def xor_psum(value, axis):
    count = lax.axis_size(axis)
    shift = 1
    while shift < count:
        partner = [(index, index ^ shift) for index in range(count)]
        value = row_major(value)
        value = value + lax.ppermute(value, axis, partner)
        shift *= 2
    return value


def halving_scatter(value, axis):
    count = lax.axis_size(axis)
    me = lax.axis_index(axis)
    shift = 1
    while shift < count:
        half = value.shape[1] // 2
        low, high = value[:, :half], value[:, half:]
        upper = (me // shift) % 2 == 1
        keep = jnp.where(upper, high, low)
        send = row_major(jnp.where(upper, low, high))
        partner = [(index, index ^ shift) for index in range(count)]
        value = keep + lax.ppermute(send, axis, partner)
        shift *= 2
    return value


def bit_reverse(value, bits):
    result = jnp.zeros_like(value)
    for bit in range(bits):
        result = result | (((value >> bit) & 1) << (bits - 1 - bit))
    return result


def near_far_reduce(value, axis, near):
    count = lax.axis_size(axis)
    me = lax.axis_index(axis)
    shift = 1
    while shift < near:
        half = value.shape[1] // 2
        low, high = value[:, :half], value[:, half:]
        upper = (me // shift) % 2 == 1
        keep = jnp.where(upper, high, low)
        send = row_major(jnp.where(upper, low, high))
        partner = [(index, index ^ shift) for index in range(count)]
        value = keep + lax.ppermute(send, axis, partner)
        shift *= 2
    while shift < count:
        value = row_major(value)
        partner = [(index, index ^ shift) for index in range(count)]
        value = value + lax.ppermute(value, axis, partner)
        shift *= 2
    return value


def doubling_gather(value, axis, shifts):
    count = lax.axis_size(axis)
    me = lax.axis_index(axis)
    for shift in shifts:
        upper = (me // shift) % 2 == 1
        value = row_major(value)
        partner = [(index, index ^ shift) for index in range(count)]
        other = lax.ppermute(value, axis, partner)
        value = jnp.where(
            upper,
            jnp.concatenate([other, value], axis=1),
            jnp.concatenate([value, other], axis=1),
        )
    return value


def near_shifts(near):
    shifts = []
    shift = near // 2
    while shift >= 1:
        shifts.append(shift)
        shift //= 2
    return shifts


def split_three(value):
    high = lax.reduce_precision(value, exponent_bits=8, mantissa_bits=7)
    rest = value - high
    middle = lax.reduce_precision(rest, exponent_bits=8, mantissa_bits=7)
    low = rest - middle
    return jnp.concatenate([high, middle, low], axis=0).astype(jnp.bfloat16)


def join_three(value):
    rows = value.shape[0] // 3
    return (value[:rows] + value[rows : 2 * rows]) + value[2 * rows :]


def group_psum(value, axis):
    count = lax.axis_size(axis)
    stride = 1
    while stride * 4 <= count:
        stride *= 4
    if stride != count:
        return xor_psum(value, axis)
    me = lax.axis_index(axis)
    stride = 1
    while stride < count:
        digit = (me // stride) % 4
        value = row_major(value)
        received = [value]
        for mate in (1, 2, 3):
            partner = [(index, index ^ (mate * stride)) for index in range(count)]
            received.append(lax.ppermute(value, axis, partner))
        stacked = jnp.stack(received)
        ordered = [stacked[member ^ digit] for member in range(4)]
        value = (ordered[0] + ordered[1]) + (ordered[2] + ordered[3])
        stride *= 4
    return value


def on_device(centroids, strengths, self_inv, wavenumbers, field_pos, targets, lists, connect):
    owned_count = centroids.shape[1]
    row_count = lax.axis_size("row")
    col_count = lax.axis_size("col")
    row_index = lax.axis_index("row")
    col_index = lax.axis_index("col")
    freqs = wavenumbers.shape[0]
    listed = lists.shape[1]
    panel_total = owned_count * row_count * col_count
    field_total = field_pos.shape[1] * row_count
    pos_rows = centroids.shape[0]
    str_rows = strengths.shape[0]
    owned = jnp.concatenate([centroids, strengths, self_inv], axis=0)
    src_all = lax.all_gather(owned, "row", axis=1, tiled=True)
    source_count = src_all.shape[1]
    panel_ids = lists.reshape(-1)
    owner_block = panel_ids // owned_count
    owner_row = owner_block // col_count
    mask = (owner_block % col_count == col_index).astype(jnp.float32)
    row_bits = max(row_count - 1, 0).bit_length()
    slot_ids = bit_reverse(owner_row, row_bits) * owned_count + panel_ids % owned_count
    slot_order = [
        sum(((slot >> bit) & 1) << (row_bits - 1 - bit) for bit in range(row_bits))
        for slot in range(row_count)
    ]
    table = src_all.reshape(-1, row_count, owned_count)
    table = jnp.concatenate([table[:, slot] for slot in slot_order], axis=1)
    src_pos = table[:pos_rows]
    src_str = table[pos_rows : pos_rows + str_rows]
    src_inv = table[pos_rows + str_rows :]
    onehot = (
        slot_ids[None, :] == lax.broadcasted_iota(jnp.int32, (source_count, slot_ids.shape[0]), 0)
    ).astype(jnp.bfloat16)
    near_all = join_three(
        jnp.dot(split_three(table[: pos_rows + str_rows]), onehot, preferred_element_type=jnp.float32)
    )
    near = near_all[:pos_rows]
    observer = jnp.repeat(field_pos, listed, axis=1)
    offset = observer - near
    distance = jnp.sqrt(jnp.sum(offset * offset, axis=0) + SOFT)
    inverse = mask / distance
    phase = wavenumbers[:, None] * distance[None]
    sine, cosine = sincos(phase)
    near_str = near_all[pos_rows:]
    str_real = near_str[:freqs]
    str_imag = near_str[freqs:]
    part_real = (cosine * str_real - sine * str_imag) * inverse
    part_imag = (cosine * str_imag + sine * str_real) * inverse
    eta_part = jnp.concatenate(
        [
            part_real.reshape(freqs, -1, listed).sum(axis=2),
            part_imag.reshape(freqs, -1, listed).sum(axis=2),
        ],
        axis=0,
    )
    eta = group_psum(eta_part, "col")
    resid = eta - targets
    rep_real = jnp.repeat(resid[:freqs], listed, axis=1)
    rep_imag = jnp.repeat(resid[freqs:], listed, axis=1)
    term_real = (cosine * rep_real + sine * rep_imag) * inverse
    term_imag = (cosine * rep_imag - sine * rep_real) * inverse
    terms = jnp.concatenate([term_real, term_imag], axis=0)
    source_part = join_three(
        lax.dot_general(
            split_three(terms),
            onehot,
            (((1,), (1,)), ((), ())),
            preferred_element_type=jnp.float32,
        )
    )
    misfit_part = jnp.sum(resid * resid)
    misfit_row = jnp.full((1, source_count), misfit_part, jnp.float32)
    near = min(8, row_count)
    chunk = near_far_reduce(jnp.concatenate([source_part, misfit_row], axis=0), "row", near)
    objective = chunk[2 * freqs, 0] / (freqs * field_total) + 1e-06
    own_slot = bit_reverse(row_index, row_bits) * owned_count
    own_offset = own_slot % chunk.shape[1]
    mu_own = complex_times(
        lax.dynamic_slice_in_dim(chunk[: 2 * freqs], own_offset, owned_count, 1) / objective,
        self_inv,
        freqs,
    )
    packed = doubling_gather(chunk, "row", near_shifts(near))
    mu_all = complex_times(packed[: 2 * freqs] / objective, src_inv, freqs)
    col_shifts = [1 << bit for bit in range(max(col_count - 1, 0).bit_length())]
    tgt_all = doubling_gather(
        jnp.concatenate([centroids, strengths, mu_own], axis=0), "col", col_shifts
    )
    tgt_pos = tgt_all[:pos_rows]
    tgt_str = tgt_all[pos_rows : pos_rows + str_rows]
    tgt_mu = tgt_all[pos_rows + str_rows :]
    block_width = tgt_pos.shape[1]
    empty = jnp.zeros((3, block_width), jnp.float32)
    accum = pair_sweep(empty, tgt_pos, tgt_str, tgt_mu, src_pos, src_str, mu_all, wavenumbers)
    panel_sens = accum * (1.0 / math.sqrt(panel_total * freqs))
    vertex_local = connect - row_index * block_width
    vertex_hits = (
        vertex_local[:, None, :] == lax.broadcasted_iota(jnp.int32, (1, block_width, 1), 1)
    ).astype(jnp.bfloat16)
    vertex_part = join_three(
        jnp.einsum(
            "cp,kvp->cv",
            split_three(0.25 * panel_sens),
            vertex_hits,
            preferred_element_type=jnp.float32,
        )
    )
    lanes = 128 if block_width % 128 == 0 else block_width
    vertex_rows = vertex_part.reshape(3 * block_width // lanes, lanes)
    vertex_sum = group_psum(vertex_rows, "col").reshape(3, block_width)
    vertex_own = lax.dynamic_slice_in_dim(vertex_sum, col_index * owned_count, owned_count, 1)
    adjoint = mu_own
    return (adjoint, vertex_own, objective)


def solution(mesh):
    return jax.shard_map(
        on_device,
        mesh=mesh,
        in_specs=(
            P(None, ("row", "col")),
            P(None, ("row", "col")),
            P(None, ("row", "col")),
            P(),
            P(None, "row"),
            P(None, "row"),
            P("row", None),
            P(None, "row"),
        ),
        out_specs=(P(None, ("row", "col")), P(None, ("row", "col")), P()),
        check_vma=False,
    )
```

```python
import math

import jax
import jax.numpy as jnp
from jax import lax
from jax.experimental.layout import Layout, with_layout_constraint
from jax.sharding import PartitionSpec as P

SOFT = 1.0


def sincos_parts(angle):
    quarter = jnp.round(angle * (2.0 / math.pi))
    rest = angle - quarter * 1.5703125
    rest = rest - quarter * 4.838267948966e-4
    rest_sq = rest * rest
    odd = rest + rest * rest_sq * (
        -1.6666654611e-1 + rest_sq * (8.3321608736e-3 + rest_sq * -1.9515295891e-4)
    )
    even = (
        1.0
        - 0.5 * rest_sq
        + rest_sq
        * rest_sq
        * (4.166664568298827e-2 + rest_sq * (-1.388731625493765e-3 + rest_sq * 2.443315711809948e-5))
    )
    return odd, even, quarter.astype(jnp.int32)


def sincos(angle):
    odd, even, turn = sincos_parts(angle)
    swap = (turn & 1) == 1
    sine = jnp.where(swap, even, odd)
    cosine = jnp.where(swap, odd, even)
    sine = jnp.where((turn & 2) == 2, -sine, sine)
    cosine = jnp.where(((turn + 1) & 2) == 2, -cosine, cosine)
    return sine, cosine


def pair_block(target_pos, target_str, target_mu, source_pos, source_str, source_mu, wavenumbers):
    freqs = wavenumbers.shape[0]
    offset = target_pos[:, None, :] - source_pos[:, :, None]
    squared = jnp.sum(offset * offset, axis=0) + SOFT
    inverse = lax.rsqrt(squared)
    distance = squared * inverse
    phase = wavenumbers[:, None, None] * distance[None]
    odd, even, turn = sincos_parts(phase)
    tgt_real = target_str[:freqs, None, :]
    tgt_imag = target_str[freqs:, None, :]
    tmu_real = target_mu[:freqs, None, :]
    tmu_imag = target_mu[freqs:, None, :]
    src_real = source_str[:freqs, :, None]
    src_imag = source_str[freqs:, :, None]
    smu_real = source_mu[:freqs, :, None]
    smu_imag = source_mu[freqs:, :, None]
    prod_real = (
        tmu_real * src_real - tmu_imag * src_imag + smu_real * tgt_real - smu_imag * tgt_imag
    )
    prod_imag = (
        tmu_real * src_imag + tmu_imag * src_real + smu_real * tgt_imag + smu_imag * tgt_real
    )
    first = prod_real + phase * prod_imag
    second = phase * prod_real - prod_imag
    swap = (turn & 1) == 1
    inner = even * jnp.where(swap, second, first) + odd * jnp.where(swap, -first, second)
    inner = jnp.where((turn & 2) == 2, inner, -inner)
    weight = jnp.sum(inner, axis=0) * (inverse * inverse * inverse)
    return jnp.sum(weight[None] * offset, axis=1)


def pair_sweep(
    total, target_pos, target_str, target_mu, source_pos, source_str, source_mu, wavenumbers
):
    width = source_pos.shape[1]
    step = math.gcd(width, 512)

    def visit_block(carry, block_index):
        begin = block_index * step
        spos = lax.dynamic_slice_in_dim(source_pos, begin, step, 1)
        sstr = lax.dynamic_slice_in_dim(source_str, begin, step, 1)
        smu = lax.dynamic_slice_in_dim(source_mu, begin, step, 1)
        return (
            carry + pair_block(target_pos, target_str, target_mu, spos, sstr, smu, wavenumbers),
            None,
        )

    result, _ = lax.scan(visit_block, total, jnp.arange(width // step, dtype=jnp.int32))
    return result


def complex_times(left, right, freqs):
    left_real, left_imag = (left[:freqs], left[freqs:])
    right_real, right_imag = (right[:freqs], right[freqs:])
    return jnp.concatenate(
        [
            left_real * right_real - left_imag * right_imag,
            left_real * right_imag + left_imag * right_real,
        ],
        axis=0,
    )


def row_major(value):
    return with_layout_constraint(value, Layout(tuple(range(value.ndim))))


def xor_psum(value, axis):
    count = lax.axis_size(axis)
    shift = 1
    while shift < count:
        partner = [(index, index ^ shift) for index in range(count)]
        value = row_major(value)
        value = value + lax.ppermute(value, axis, partner)
        shift *= 2
    return value


def halving_scatter(value, axis):
    count = lax.axis_size(axis)
    me = lax.axis_index(axis)
    shift = 1
    while shift < count:
        half = value.shape[1] // 2
        low, high = value[:, :half], value[:, half:]
        upper = (me // shift) % 2 == 1
        keep = jnp.where(upper, high, low)
        send = row_major(jnp.where(upper, low, high))
        partner = [(index, index ^ shift) for index in range(count)]
        value = keep + lax.ppermute(send, axis, partner)
        shift *= 2
    return value


def bit_reverse(value, bits):
    result = jnp.zeros_like(value)
    for bit in range(bits):
        result = result | (((value >> bit) & 1) << (bits - 1 - bit))
    return result


def near_far_reduce(value, axis, near):
    count = lax.axis_size(axis)
    me = lax.axis_index(axis)
    shift = 1
    while shift < near:
        half = value.shape[1] // 2
        low, high = value[:, :half], value[:, half:]
        upper = (me // shift) % 2 == 1
        keep = jnp.where(upper, high, low)
        send = row_major(jnp.where(upper, low, high))
        partner = [(index, index ^ shift) for index in range(count)]
        value = keep + lax.ppermute(send, axis, partner)
        shift *= 2
    while shift < count:
        value = row_major(value)
        partner = [(index, index ^ shift) for index in range(count)]
        value = value + lax.ppermute(value, axis, partner)
        shift *= 2
    return value


def doubling_gather(value, axis, shifts):
    count = lax.axis_size(axis)
    me = lax.axis_index(axis)
    for shift in shifts:
        upper = (me // shift) % 2 == 1
        value = row_major(value)
        partner = [(index, index ^ shift) for index in range(count)]
        other = lax.ppermute(value, axis, partner)
        value = jnp.where(
            upper,
            jnp.concatenate([other, value], axis=1),
            jnp.concatenate([value, other], axis=1),
        )
    return value


def near_shifts(near):
    shifts = []
    shift = near // 2
    while shift >= 1:
        shifts.append(shift)
        shift //= 2
    return shifts


def split_three(value):
    high = lax.reduce_precision(value, exponent_bits=8, mantissa_bits=7)
    rest = value - high
    middle = lax.reduce_precision(rest, exponent_bits=8, mantissa_bits=7)
    low = rest - middle
    return jnp.concatenate([high, middle, low], axis=0).astype(jnp.bfloat16)


def join_three(value):
    rows = value.shape[0] // 3
    return (value[:rows] + value[rows : 2 * rows]) + value[2 * rows :]


def on_device(centroids, strengths, self_inv, wavenumbers, field_pos, targets, lists, connect):
    owned_count = centroids.shape[1]
    row_count = lax.axis_size("row")
    col_count = lax.axis_size("col")
    row_index = lax.axis_index("row")
    col_index = lax.axis_index("col")
    freqs = wavenumbers.shape[0]
    listed = lists.shape[1]
    panel_total = owned_count * row_count * col_count
    field_total = field_pos.shape[1] * row_count
    pos_rows = centroids.shape[0]
    str_rows = strengths.shape[0]
    owned = jnp.concatenate([centroids, strengths, self_inv], axis=0)
    src_all = lax.all_gather(owned, "row", axis=1, tiled=True)
    source_count = src_all.shape[1]
    panel_ids = lists.reshape(-1)
    owner_block = panel_ids // owned_count
    owner_row = owner_block // col_count
    mask = (owner_block % col_count == col_index).astype(jnp.float32)
    row_bits = max(row_count - 1, 0).bit_length()
    slot_ids = bit_reverse(owner_row, row_bits) * owned_count + panel_ids % owned_count
    slot_order = [
        sum(((slot >> bit) & 1) << (row_bits - 1 - bit) for bit in range(row_bits))
        for slot in range(row_count)
    ]
    table = src_all.reshape(-1, row_count, owned_count)
    table = jnp.concatenate([table[:, slot] for slot in slot_order], axis=1)
    src_pos = table[:pos_rows]
    src_str = table[pos_rows : pos_rows + str_rows]
    src_inv = table[pos_rows + str_rows :]
    onehot = (
        slot_ids[None, :] == lax.broadcasted_iota(jnp.int32, (source_count, slot_ids.shape[0]), 0)
    ).astype(jnp.bfloat16)
    near_all = join_three(
        jnp.dot(split_three(table[: pos_rows + str_rows]), onehot, preferred_element_type=jnp.float32)
    )
    near = near_all[:pos_rows]
    observer = jnp.repeat(field_pos, listed, axis=1)
    offset = observer - near
    distance = jnp.sqrt(jnp.sum(offset * offset, axis=0) + SOFT)
    inverse = mask / distance
    phase = wavenumbers[:, None] * distance[None]
    sine, cosine = sincos(phase)
    near_str = near_all[pos_rows:]
    str_real = near_str[:freqs]
    str_imag = near_str[freqs:]
    part_real = (cosine * str_real - sine * str_imag) * inverse
    part_imag = (cosine * str_imag + sine * str_real) * inverse
    point_count = field_pos.shape[1]
    point_hits = (
        lax.broadcasted_iota(jnp.int32, (point_count * listed, point_count), 0) // listed
        == lax.broadcasted_iota(jnp.int32, (point_count * listed, point_count), 1)
    ).astype(jnp.bfloat16)
    eta_part = join_three(
        jnp.dot(
            split_three(jnp.concatenate([part_real, part_imag], axis=0)),
            point_hits,
            preferred_element_type=jnp.float32,
        )
    )
    eta = xor_psum(eta_part, "col")
    resid = eta - targets
    rep_real = jnp.repeat(resid[:freqs], listed, axis=1)
    rep_imag = jnp.repeat(resid[freqs:], listed, axis=1)
    term_real = (cosine * rep_real + sine * rep_imag) * inverse
    term_imag = (cosine * rep_imag - sine * rep_real) * inverse
    terms = jnp.concatenate([term_real, term_imag], axis=0)
    source_part = join_three(
        lax.dot_general(
            split_three(terms),
            onehot,
            (((1,), (1,)), ((), ())),
            preferred_element_type=jnp.float32,
        )
    )
    misfit_part = jnp.sum(resid * resid)
    misfit_row = jnp.full((1, source_count), misfit_part, jnp.float32)
    near = min(8, row_count)
    chunk = near_far_reduce(jnp.concatenate([source_part, misfit_row], axis=0), "row", near)
    objective = chunk[2 * freqs, 0] / (freqs * field_total) + 1e-06
    own_slot = bit_reverse(row_index, row_bits) * owned_count
    own_offset = own_slot % chunk.shape[1]
    mu_own = complex_times(
        lax.dynamic_slice_in_dim(chunk[: 2 * freqs], own_offset, owned_count, 1) / objective,
        self_inv,
        freqs,
    )
    packed = doubling_gather(chunk, "row", near_shifts(near))
    mu_all = complex_times(packed[: 2 * freqs] / objective, src_inv, freqs)
    col_shifts = [1 << bit for bit in range(max(col_count - 1, 0).bit_length())]
    tgt_all = doubling_gather(
        jnp.concatenate([centroids, strengths, mu_own], axis=0), "col", col_shifts
    )
    tgt_pos = tgt_all[:pos_rows]
    tgt_str = tgt_all[pos_rows : pos_rows + str_rows]
    tgt_mu = tgt_all[pos_rows + str_rows :]
    block_width = tgt_pos.shape[1]
    empty = jnp.zeros((3, block_width), jnp.float32)
    accum = pair_sweep(empty, tgt_pos, tgt_str, tgt_mu, src_pos, src_str, mu_all, wavenumbers)
    panel_sens = accum * (1.0 / math.sqrt(panel_total * freqs))
    vertex_local = connect - row_index * block_width
    vertex_hits = (
        vertex_local[:, None, :] == lax.broadcasted_iota(jnp.int32, (1, block_width, 1), 1)
    ).astype(jnp.bfloat16)
    vertex_part = join_three(
        jnp.einsum(
            "cp,kvp->cv",
            split_three(0.25 * panel_sens),
            vertex_hits,
            preferred_element_type=jnp.float32,
        )
    )
    lanes = 128 if block_width % 128 == 0 else block_width
    vertex_rows = vertex_part.reshape(3 * block_width // lanes, lanes)
    vertex_sum = xor_psum(vertex_rows, "col").reshape(3, block_width)
    vertex_own = lax.dynamic_slice_in_dim(vertex_sum, col_index * owned_count, owned_count, 1)
    adjoint = mu_own
    return (adjoint, vertex_own, objective)


def solution(mesh):
    return jax.shard_map(
        on_device,
        mesh=mesh,
        in_specs=(
            P(None, ("row", "col")),
            P(None, ("row", "col")),
            P(None, ("row", "col")),
            P(),
            P(None, "row"),
            P(None, "row"),
            P("row", None),
            P(None, "row"),
        ),
        out_specs=(P(None, ("row", "col")), P(None, ("row", "col")), P()),
        check_vma=False,
    )
```

```python
import math

import jax
import jax.numpy as jnp
from jax import lax
from jax.experimental.layout import Layout, with_layout_constraint
from jax.sharding import PartitionSpec as P

SOFT = 1.0


def sincos_parts(angle):
    quarter = jnp.round(angle * (2.0 / math.pi))
    rest = angle - quarter * 1.5703125
    rest = rest - quarter * 4.838267948966e-4
    rest_sq = rest * rest
    odd = rest + rest * rest_sq * (
        -1.6666654611e-1 + rest_sq * (8.3321608736e-3 + rest_sq * -1.9515295891e-4)
    )
    even = (
        1.0
        - 0.5 * rest_sq
        + rest_sq
        * rest_sq
        * (4.166664568298827e-2 + rest_sq * (-1.388731625493765e-3 + rest_sq * 2.443315711809948e-5))
    )
    return odd, even, quarter.astype(jnp.int32)


def sincos(angle):
    odd, even, turn = sincos_parts(angle)
    swap = (turn & 1) == 1
    sine = jnp.where(swap, even, odd)
    cosine = jnp.where(swap, odd, even)
    sine = jnp.where((turn & 2) == 2, -sine, sine)
    cosine = jnp.where(((turn + 1) & 2) == 2, -cosine, cosine)
    return sine, cosine


def pair_block(target_pos, target_str, target_mu, source_pos, source_str, source_mu, wavenumbers):
    freqs = wavenumbers.shape[0]
    offset = target_pos[:, None, :] - source_pos[:, :, None]
    squared = jnp.sum(offset * offset, axis=0) + SOFT
    inverse = lax.rsqrt(squared)
    distance = squared * inverse
    phase = wavenumbers[:, None, None] * distance[None]
    odd, even, turn = sincos_parts(phase)
    tgt_real = target_str[:freqs, None, :]
    tgt_imag = target_str[freqs:, None, :]
    tmu_real = target_mu[:freqs, None, :]
    tmu_imag = target_mu[freqs:, None, :]
    src_real = source_str[:freqs, :, None]
    src_imag = source_str[freqs:, :, None]
    smu_real = source_mu[:freqs, :, None]
    smu_imag = source_mu[freqs:, :, None]
    prod_real = (
        tmu_real * src_real - tmu_imag * src_imag + smu_real * tgt_real - smu_imag * tgt_imag
    )
    prod_imag = (
        tmu_real * src_imag + tmu_imag * src_real + smu_real * tgt_imag + smu_imag * tgt_real
    )
    first = prod_real + phase * prod_imag
    second = phase * prod_real - prod_imag
    swap = (turn & 1) == 1
    inner = even * jnp.where(swap, second, first) + odd * jnp.where(swap, -first, second)
    inner = jnp.where((turn & 2) == 2, inner, -inner)
    weight = jnp.sum(inner, axis=0) * (inverse * inverse * inverse)
    return jnp.sum(weight[None] * offset, axis=1)


def pair_sweep(
    total, target_pos, target_str, target_mu, source_pos, source_str, source_mu, wavenumbers
):
    width = source_pos.shape[1]
    step = math.gcd(width, 1024)

    def visit_block(carry, block_index):
        begin = block_index * step
        spos = lax.dynamic_slice_in_dim(source_pos, begin, step, 1)
        sstr = lax.dynamic_slice_in_dim(source_str, begin, step, 1)
        smu = lax.dynamic_slice_in_dim(source_mu, begin, step, 1)
        return (
            carry + pair_block(target_pos, target_str, target_mu, spos, sstr, smu, wavenumbers),
            None,
        )

    result, _ = lax.scan(visit_block, total, jnp.arange(width // step, dtype=jnp.int32))
    return result


def complex_times(left, right, freqs):
    left_real, left_imag = (left[:freqs], left[freqs:])
    right_real, right_imag = (right[:freqs], right[freqs:])
    return jnp.concatenate(
        [
            left_real * right_real - left_imag * right_imag,
            left_real * right_imag + left_imag * right_real,
        ],
        axis=0,
    )


def row_major(value):
    return with_layout_constraint(value, Layout(tuple(range(value.ndim))))


def xor_psum(value, axis):
    count = lax.axis_size(axis)
    shift = 1
    while shift < count:
        partner = [(index, index ^ shift) for index in range(count)]
        value = row_major(value)
        value = value + lax.ppermute(value, axis, partner)
        shift *= 2
    return value


def halving_scatter(value, axis):
    count = lax.axis_size(axis)
    me = lax.axis_index(axis)
    shift = 1
    while shift < count:
        half = value.shape[1] // 2
        low, high = value[:, :half], value[:, half:]
        upper = (me // shift) % 2 == 1
        keep = jnp.where(upper, high, low)
        send = row_major(jnp.where(upper, low, high))
        partner = [(index, index ^ shift) for index in range(count)]
        value = keep + lax.ppermute(send, axis, partner)
        shift *= 2
    return value


def bit_reverse(value, bits):
    result = jnp.zeros_like(value)
    for bit in range(bits):
        result = result | (((value >> bit) & 1) << (bits - 1 - bit))
    return result


def near_far_reduce(value, axis, near):
    count = lax.axis_size(axis)
    me = lax.axis_index(axis)
    shift = 1
    while shift < near:
        half = value.shape[1] // 2
        low, high = value[:, :half], value[:, half:]
        upper = (me // shift) % 2 == 1
        keep = jnp.where(upper, high, low)
        send = row_major(jnp.where(upper, low, high))
        partner = [(index, index ^ shift) for index in range(count)]
        value = keep + lax.ppermute(send, axis, partner)
        shift *= 2
    while shift < count:
        value = row_major(value)
        partner = [(index, index ^ shift) for index in range(count)]
        value = value + lax.ppermute(value, axis, partner)
        shift *= 2
    return value


def doubling_gather(value, axis, shifts):
    count = lax.axis_size(axis)
    me = lax.axis_index(axis)
    for shift in shifts:
        upper = (me // shift) % 2 == 1
        value = row_major(value)
        partner = [(index, index ^ shift) for index in range(count)]
        other = lax.ppermute(value, axis, partner)
        value = jnp.where(
            upper,
            jnp.concatenate([other, value], axis=1),
            jnp.concatenate([value, other], axis=1),
        )
    return value


def near_shifts(near):
    shifts = []
    shift = near // 2
    while shift >= 1:
        shifts.append(shift)
        shift //= 2
    return shifts


def split_three(value):
    high = lax.reduce_precision(value, exponent_bits=8, mantissa_bits=7)
    rest = value - high
    middle = lax.reduce_precision(rest, exponent_bits=8, mantissa_bits=7)
    low = rest - middle
    return jnp.concatenate([high, middle, low], axis=0).astype(jnp.bfloat16)


def join_three(value):
    rows = value.shape[0] // 3
    return (value[:rows] + value[rows : 2 * rows]) + value[2 * rows :]


def on_device(centroids, strengths, self_inv, wavenumbers, field_pos, targets, lists, connect):
    owned_count = centroids.shape[1]
    row_count = lax.axis_size("row")
    col_count = lax.axis_size("col")
    row_index = lax.axis_index("row")
    col_index = lax.axis_index("col")
    freqs = wavenumbers.shape[0]
    listed = lists.shape[1]
    panel_total = owned_count * row_count * col_count
    field_total = field_pos.shape[1] * row_count
    pos_rows = centroids.shape[0]
    str_rows = strengths.shape[0]
    owned = jnp.concatenate([centroids, strengths, self_inv], axis=0)
    src_all = lax.all_gather(owned, "row", axis=1, tiled=True)
    source_count = src_all.shape[1]
    panel_ids = lists.reshape(-1)
    owner_block = panel_ids // owned_count
    owner_row = owner_block // col_count
    mask = (owner_block % col_count == col_index).astype(jnp.float32)
    row_bits = max(row_count - 1, 0).bit_length()
    slot_ids = bit_reverse(owner_row, row_bits) * owned_count + panel_ids % owned_count
    slot_order = [
        sum(((slot >> bit) & 1) << (row_bits - 1 - bit) for bit in range(row_bits))
        for slot in range(row_count)
    ]
    table = src_all.reshape(-1, row_count, owned_count)
    table = jnp.concatenate([table[:, slot] for slot in slot_order], axis=1)
    src_pos = table[:pos_rows]
    src_str = table[pos_rows : pos_rows + str_rows]
    src_inv = table[pos_rows + str_rows :]
    onehot = (
        slot_ids[None, :] == lax.broadcasted_iota(jnp.int32, (source_count, slot_ids.shape[0]), 0)
    ).astype(jnp.bfloat16)
    near_all = join_three(
        jnp.dot(split_three(table[: pos_rows + str_rows]), onehot, preferred_element_type=jnp.float32)
    )
    near = near_all[:pos_rows]
    observer = jnp.repeat(field_pos, listed, axis=1)
    offset = observer - near
    distance = jnp.sqrt(jnp.sum(offset * offset, axis=0) + SOFT)
    inverse = mask / distance
    phase = wavenumbers[:, None] * distance[None]
    sine, cosine = sincos(phase)
    near_str = near_all[pos_rows:]
    str_real = near_str[:freqs]
    str_imag = near_str[freqs:]
    part_real = (cosine * str_real - sine * str_imag) * inverse
    part_imag = (cosine * str_imag + sine * str_real) * inverse
    eta_part = jnp.concatenate(
        [
            part_real.reshape(freqs, -1, listed).sum(axis=2),
            part_imag.reshape(freqs, -1, listed).sum(axis=2),
        ],
        axis=0,
    )
    eta = xor_psum(eta_part, "col")
    resid = eta - targets
    rep_real = jnp.repeat(resid[:freqs], listed, axis=1)
    rep_imag = jnp.repeat(resid[freqs:], listed, axis=1)
    term_real = (cosine * rep_real + sine * rep_imag) * inverse
    term_imag = (cosine * rep_imag - sine * rep_real) * inverse
    terms = jnp.concatenate([term_real, term_imag], axis=0)
    source_part = join_three(
        lax.dot_general(
            split_three(terms),
            onehot,
            (((1,), (1,)), ((), ())),
            preferred_element_type=jnp.float32,
        )
    )
    misfit_part = jnp.sum(resid * resid)
    misfit_row = jnp.full((1, source_count), misfit_part, jnp.float32)
    near = min(8, row_count)
    chunk = near_far_reduce(jnp.concatenate([source_part, misfit_row], axis=0), "row", near)
    objective = chunk[2 * freqs, 0] / (freqs * field_total) + 1e-06
    own_slot = bit_reverse(row_index, row_bits) * owned_count
    own_offset = own_slot % chunk.shape[1]
    mu_own = complex_times(
        lax.dynamic_slice_in_dim(chunk[: 2 * freqs], own_offset, owned_count, 1) / objective,
        self_inv,
        freqs,
    )
    packed = doubling_gather(chunk, "row", near_shifts(near))
    mu_all = complex_times(packed[: 2 * freqs] / objective, src_inv, freqs)
    col_shifts = [1 << bit for bit in range(max(col_count - 1, 0).bit_length())]
    tgt_all = doubling_gather(
        jnp.concatenate([centroids, strengths, mu_own], axis=0), "col", col_shifts
    )
    tgt_pos = tgt_all[:pos_rows]
    tgt_str = tgt_all[pos_rows : pos_rows + str_rows]
    tgt_mu = tgt_all[pos_rows + str_rows :]
    block_width = tgt_pos.shape[1]
    empty = jnp.zeros((3, block_width), jnp.float32)
    accum = pair_sweep(empty, tgt_pos, tgt_str, tgt_mu, src_pos, src_str, mu_all, wavenumbers)
    panel_sens = accum * (1.0 / math.sqrt(panel_total * freqs))
    vertex_local = connect - row_index * block_width
    vertex_hits = (
        vertex_local[:, None, :] == lax.broadcasted_iota(jnp.int32, (1, block_width, 1), 1)
    ).astype(jnp.bfloat16)
    vertex_part = join_three(
        jnp.einsum(
            "cp,kvp->cv",
            split_three(0.25 * panel_sens),
            vertex_hits,
            preferred_element_type=jnp.float32,
        )
    )
    lanes = 128 if block_width % 128 == 0 else block_width
    vertex_rows = vertex_part.reshape(3 * block_width // lanes, lanes)
    vertex_sum = xor_psum(vertex_rows, "col").reshape(3, block_width)
    vertex_own = lax.dynamic_slice_in_dim(vertex_sum, col_index * owned_count, owned_count, 1)
    adjoint = mu_own
    return (adjoint, vertex_own, objective)


def solution(mesh):
    return jax.shard_map(
        on_device,
        mesh=mesh,
        in_specs=(
            P(None, ("row", "col")),
            P(None, ("row", "col")),
            P(None, ("row", "col")),
            P(),
            P(None, "row"),
            P(None, "row"),
            P("row", None),
            P(None, "row"),
        ),
        out_specs=(P(None, ("row", "col")), P(None, ("row", "col")), P()),
        check_vma=False,
    )
```
